256 devices in a mesh: ta: 4 (over z_lo), row: 16 (over y, z_hi, core), col: 4 (over x).
Axes of the slice: x: 4, y: 4, z: 8 (z_hi: 2, z_lo: 4; z = z_hi * 4 + z_lo), core: 2. Of those that a mesh axis runs over, the one named last changes fastest.
Arguments:
- features: bfloat16 [32, 96, 128, 256], P(None, None, 'row', ('ta', 'col')), may hold values from -6 to 6
- conv_weight: bfloat16 [3, 3, 96, 96], replicated, may hold values from -0.21875 to 0.21875
- time_weight: float32 [96, 5], replicated, may hold values from -2.5 to 2.5
- band_out: bfloat16 [96, 28], replicated, may hold values from -0.625 to 0.625
- band_input_weight: bfloat16 [28, 96], replicated, may hold values from -0.25 to 0.25
- measured: float32 [32, 128, 310], P(('ta', 'col'), 'row'), may hold values from -24 to 24
- aperture: int32 [32, 128, 256], P(('ta', 'col'), 'row'), may hold values 0 or 1
- dispersion: int32 [28], replicated, may hold values from 0 to 54, as said below
- update_cot: bfloat16 [32, 96, 128, 256], P(('ta', 'col'), None, 'row'), may hold values from -6 to 6
Outputs:
- updated: bfloat16 [32, 96, 128, 256], P(('ta', 'col'), None, 'row')
- features_grad: bfloat16 [32, 96, 128, 256], P(None, None, 'row', ('ta', 'col'))
The draws below stay inside these ranges and needn't reach their ends.
Inputs may be any that keep to these rules, and one draw needn't show every extreme that they name: `dispersion`: some band has shift 0 and some band shift 54.
All inputs are finite; a program needn't handle non-finite values. No bound on the sum of `aperture` on one device may be relied on, other than what follows from the above.
Results may differ from the reference program's by a relative error of at most 0.0059.
Values may be sent and summed in bfloat16 or wider, within the bound.
No kernel may reach another device: no remote copies, remote signals or barrier semaphores. Data moves between devices by JAX's collectives and lax.ppermute only.
A program may use at most 128 MiB of HBM per device.

```python
import jax
import jax.numpy as jnp
from jax import lax

C = 96
B = 28
SMAX = 54
F = 32
H = 128
W = 256
WM = 310


def draw_dispersion(key, part):
    drawn = jax.random.randint(key, (B,), 0, SMAX + 1)
    position = jnp.arange(B)
    drawn = jnp.where(position == 0, 0, drawn)
    drawn = jnp.where(position == B - 1, SMAX, drawn)
    return drawn.astype(jnp.int32)


def set_ends(entries, own_key, smallest, high):
    shape = entries.shape
    index_at = [jax.random.randint(jax.random.fold_in(own_key, axis), (), 0, shape[axis]) for axis in range(len(shape))]
    entries = entries.at[tuple(index_at)].set(smallest)
    longest = shape.index(max(shape))
    index_at[longest] = (index_at[longest] + 1) % shape[longest]
    return entries.at[tuple(index_at)].set(high)


def steps_of(stream_key, dims, pieces, smallest, largest):
    level = 1.0
    for axis_at, shards_of in pieces:
        heights = jax.random.uniform(jax.random.fold_in(jax.random.fold_in(stream_key, 6), axis_at), (shards_of,), jnp.float32, smallest / len(pieces), largest / len(pieces))
        level = level * jnp.repeat(jnp.exp(heights), dims[axis_at] // shards_of).reshape((-1,) + (1,) * (len(dims) - 1 - axis_at))
    return level


def normal_values(rng, extent, deviation, most, split=(), kind=jnp.bfloat16):
    array = deviation * jax.random.normal(rng, extent, jnp.float32)
    if split:
        array = array * steps_of(rng, extent, split, -0.22, 0.18)
    return jnp.clip(array, -most, most).astype(kind)


def setup_inputs(seed: int = 0) -> dict:
    seeds = jax.random.split(jax.random.key(seed), 10)
    return {
        "features": normal_values(seeds[0], (F, C, H, W), 1.0, 6.0, ((2, 16), (3, 16))),
        "conv_weight": normal_values(seeds[1], (3, 3, C, C), (9 * C) ** -0.5, 0.21875),
        "time_weight": normal_values(seeds[2], (C, 5), 5 ** -0.5, 2.5, (), jnp.float32),
        "band_out": normal_values(seeds[3], (C, B), C ** -0.5, 0.625),
        "band_input_weight": normal_values(seeds[4], (B, C), (16 * B) ** -0.5, 0.25),
        "measured": normal_values(seeds[5], (F, H, WM), 4.0, 24.0, ((0, 16), (1, 16)), jnp.float32),
        "aperture": set_ends((jax.random.randint(seeds[6], (F, H, W), 0, 2) < 1).astype(jnp.int32), jax.random.fold_in(seeds[6], 1), 0, 1),
        "dispersion": draw_dispersion(jax.random.fold_in(seeds[9], 71), 0),
        "update_cot": normal_values(seeds[8], (F, C, H, W), 1.0, 6.0, ((0, 16), (2, 16))),
    }


def conv_frame(picture, kernel):
    row_number = picture.shape[1]
    col_count = picture.shape[2]
    padded = jnp.pad(picture.astype(jnp.float32), ((0, 0), (1, 1), (1, 1)))
    weights = kernel.astype(jnp.float32)
    summed = jnp.zeros((kernel.shape[3], row_number, col_count), jnp.float32)
    for row_tap in range(3):
        for col_tap in range(3):
            window = padded[:, row_tap:row_tap + row_number, col_tap:col_tap + col_count]
            summed = summed + jnp.einsum('iqw,io->oqw', window, weights[row_tap, col_tap])
    return summed

def disperse(masked, dispersion, extra_cols):
    band_axis = masked.ndim - 3
    widened = jnp.pad(masked, [(0, 0)] * (masked.ndim - 1) + [(0, extra_cols)])

    def move_one(band_plane, offset):
        return jnp.roll(band_plane, offset, axis=-1)
    shifted = jax.vmap(move_one, in_axes=(band_axis, 0), out_axes=band_axis)(widened, dispersion)
    return lax.optimization_barrier(jnp.sum(shifted, axis=band_axis))

def undisperse(field_in, dispersion, width_keep):

    def take_one(offset):
        return jnp.roll(field_in, -offset, axis=-1)[..., :width_keep]
    return jax.vmap(take_one, out_axes=field_in.ndim - 2)(dispersion)

def time_mix(window, time_taps):
    summed = jnp.zeros(window.shape[1:], jnp.float32)
    for tap_index in range(5):
        summed = summed + time_taps[:, tap_index, None, None] * window[tap_index].astype(jnp.float32)
    return summed

def gelu_exact(values_in):
    return jax.nn.gelu(values_in, approximate=False)

def reference(features, conv_weight, time_weight, band_out, band_input_weight, measured, aperture, dispersion, update_cot):

    def segment_one(picture):
        pre_act = conv_frame(picture, conv_weight)
        return (picture.astype(jnp.float32) + gelu_exact(pre_act)).astype(jnp.bfloat16)
    hidden_state = lax.map(segment_one, features)
    padded_hidden = jnp.pad(hidden_state, ((2, 2), (0, 0), (0, 0), (0, 0)))
    time_taps = time_weight.astype(jnp.float32)
    out_proj = band_out.astype(jnp.float32)
    in_proj = band_input_weight.astype(jnp.float32)

    def segment_two(frame_index):
        window = lax.dynamic_slice_in_dim(padded_hidden, frame_index, 5, 0)
        temporal = time_mix(window, time_taps).astype(jnp.bfloat16)
        mask_float = lax.dynamic_index_in_dim(aperture, frame_index, 0, False).astype(jnp.float32)
        measured_image = lax.dynamic_index_in_dim(measured, frame_index, 0, False)
        cot_frame = lax.dynamic_index_in_dim(update_cot, frame_index, 0, False).astype(jnp.float32)
        band_vals = jnp.einsum('cqw,cb->bqw', temporal.astype(jnp.float32), out_proj)
        masked_band_sum = disperse(band_vals * mask_float, dispersion, SMAX)
        residual_error = measured_image - masked_band_sum
        back_proj = (undisperse(residual_error, dispersion, W) * mask_float).astype(jnp.bfloat16)
        updated = (temporal.astype(jnp.float32) + jnp.einsum('bqw,bc->cqw', back_proj.astype(jnp.float32), in_proj)).astype(jnp.bfloat16)
        band_cot = jnp.einsum('cqw,bc->bqw', cot_frame, in_proj)
        resid_grad = disperse(band_cot * mask_float, dispersion, SMAX)
        band_grad = (-(undisperse(resid_grad, dispersion, W) * mask_float)).astype(jnp.bfloat16)
        cot_temporal = (cot_frame + jnp.einsum('bqw,cb->cqw', band_grad.astype(jnp.float32), out_proj)).astype(jnp.bfloat16)
        return (updated, cot_temporal)
    updated, cot_temporal = lax.map(segment_two, jnp.arange(F, dtype=jnp.int32))
    padded_cot = jnp.pad(cot_temporal, ((2, 2), (0, 0), (0, 0), (0, 0)))
    flipped = time_taps[:, ::-1]
    kernel_flip = jnp.transpose(conv_weight[::-1, ::-1], (0, 1, 3, 2))

    def segment_three(frame_index):
        window = lax.dynamic_slice_in_dim(padded_cot, frame_index, 5, 0)
        cot_hidden = time_mix(window, flipped).astype(jnp.bfloat16)
        picture = lax.dynamic_index_in_dim(features, frame_index, 0, False)
        pre_act = conv_frame(picture, conv_weight)
        pullback = jax.vjp(gelu_exact, pre_act)[1]
        gate_grad = pullback(cot_hidden.astype(jnp.float32))[0].astype(jnp.bfloat16)
        return (cot_hidden.astype(jnp.float32) + conv_frame(gate_grad, kernel_flip)).astype(jnp.bfloat16)
    features_grad = lax.map(segment_three, jnp.arange(F, dtype=jnp.int32))
    return (updated, features_grad)
```

```python
import jax
import jax.numpy as jnp
from jax import lax
from jax.sharding import PartitionSpec as P


def with_halo(array, sides, width):
    for axis, dim in sides:
        devices, length = (lax.axis_size(axis), array.shape[dim])
        up = [(i, (i + 1) % devices) for i in range(devices - 1)]
        down = [(j, i) for i, j in up]
        last = lax.slice_in_dim(array, length - width, length, axis=dim)
        initial = lax.slice_in_dim(array, 0, width, axis=dim)
        before = lax.ppermute(last, axis, up)
        after = lax.ppermute(initial, axis, down)
        array = jnp.concatenate([before, array, after], axis=dim)
    return array


def spatial_conv(field_in, kernel):
    padded = with_halo(field_in, (("row", 2), (("ta", "col"), 3)), 1)
    return lax.conv_general_dilated(
        padded,
        kernel,
        window_strides=(1, 1),
        padding="VALID",
        dimension_numbers=("NCHW", "HWIO", "NCHW"),
        preferred_element_type=jnp.float32,
    )


def to_time(field_in):
    return lax.all_to_all(field_in, ("ta", "col"), split_axis=0, concat_axis=3, tiled=True)


def to_space(field_in):
    return lax.all_to_all(field_in, ("ta", "col"), split_axis=3, concat_axis=0, tiled=True)


def time_mix(frames_in, time_taps):
    frame_count = frames_in.shape[0]
    padded = jnp.pad(frames_in, ((2, 2), (0, 0), (0, 0), (0, 0)))
    summed = jnp.zeros(frames_in.shape, jnp.float32)
    for tap_index in range(5):
        summed = summed + time_taps[None, :, tap_index, None, None] * padded[
            tap_index : tap_index + frame_count
        ].astype(jnp.float32)
    return summed


def gelu_exact(values_in):
    return jax.nn.gelu(values_in, approximate=False)


def shift_table(dispersion, width_keep, width_wide):
    source_col = lax.broadcasted_iota(jnp.int32, (1, width_keep, width_wide), 1)
    target_col = lax.broadcasted_iota(jnp.int32, (1, width_keep, width_wide), 2)
    return (target_col == source_col + dispersion[:, None, None]).astype(jnp.float32)


def disperse(masked, table):
    return jnp.einsum(
        "fbqw,bwv->fqv",
        masked,
        table,
        precision=lax.Precision.HIGHEST,
        preferred_element_type=jnp.float32,
    )


def undisperse(field_in, table):
    return jnp.einsum(
        "fqv,bwv->fbqw",
        field_in,
        table,
        precision=lax.Precision.HIGHEST,
        preferred_element_type=jnp.float32,
    )


def on_device(
    features,
    conv_weight,
    time_weight,
    band_out,
    band_input_weight,
    measured,
    aperture,
    dispersion,
    update_cot,
):
    pre_act = spatial_conv(features, conv_weight)
    hidden_state = (features.astype(jnp.float32) + gelu_exact(pre_act)).astype(jnp.bfloat16)
    temporal = to_time(time_mix(hidden_state, time_weight).astype(jnp.bfloat16))
    width_keep = aperture.shape[-1]
    width_wide = measured.shape[-1]
    table = shift_table(dispersion, width_keep, width_wide)
    mask_float = aperture.astype(jnp.float32)[:, None]
    band_vals = jnp.einsum("fcqw,cb->fbqw", temporal, band_out, preferred_element_type=jnp.float32)
    masked_band_sum = disperse(band_vals * mask_float, table)
    residual_error = measured - masked_band_sum
    back_proj = (undisperse(residual_error, table) * mask_float).astype(jnp.bfloat16)
    updated = (
        temporal.astype(jnp.float32)
        + jnp.einsum(
            "fbqw,bc->fcqw", back_proj, band_input_weight, preferred_element_type=jnp.float32
        )
    ).astype(jnp.bfloat16)
    band_cot = jnp.einsum(
        "fcqw,bc->fbqw", update_cot, band_input_weight, preferred_element_type=jnp.float32
    )
    resid_grad = disperse(band_cot * mask_float, table)
    band_grad = (-(undisperse(resid_grad, table) * mask_float)).astype(jnp.bfloat16)
    cot_temporal = (
        update_cot.astype(jnp.float32)
        + jnp.einsum("fbqw,cb->fcqw", band_grad, band_out, preferred_element_type=jnp.float32)
    ).astype(jnp.bfloat16)
    flipped = time_weight[:, ::-1]
    cot_hidden = time_mix(to_space(cot_temporal), flipped).astype(jnp.bfloat16)
    pullback = jax.vjp(gelu_exact, pre_act)[1]
    gate_grad = pullback(cot_hidden.astype(jnp.float32))[0].astype(jnp.bfloat16)
    kernel_flip = jnp.transpose(conv_weight[::-1, ::-1], (0, 1, 3, 2))
    features_grad = (cot_hidden.astype(jnp.float32) + spatial_conv(gate_grad, kernel_flip)).astype(
        jnp.bfloat16
    )
    return (updated, features_grad)


def solution(mesh):
    return jax.shard_map(
        on_device,
        mesh=mesh,
        in_specs=(
            P(None, None, "row", ("ta", "col")),
            P(),
            P(),
            P(),
            P(),
            P(("ta", "col"), "row", None),
            P(("ta", "col"), "row", None),
            P(),
            P(("ta", "col"), None, "row", None),
        ),
        out_specs=(P(("ta", "col"), None, "row", None), P(None, None, "row", ("ta", "col"))),
        check_vma=False,
    )
```

```python
import jax
import jax.numpy as jnp
from jax import lax
from jax.sharding import PartitionSpec as P


def with_halo(array, sides, width):
    for axis, dim in sides:
        devices, length = (lax.axis_size(axis), array.shape[dim])
        up = [(i, (i + 1) % devices) for i in range(devices - 1)]
        down = [(j, i) for i, j in up]
        last = lax.slice_in_dim(array, length - width, length, axis=dim)
        initial = lax.slice_in_dim(array, 0, width, axis=dim)
        before = lax.ppermute(last, axis, up)
        after = lax.ppermute(initial, axis, down)
        array = jnp.concatenate([before, array, after], axis=dim)
    return array


def valid_conv(padded, kernel):
    return lax.conv_general_dilated(
        padded,
        kernel,
        window_strides=(1, 1),
        padding="VALID",
        dimension_numbers=("NCHW", "HWIO", "NCHW"),
        preferred_element_type=jnp.float32,
    )


def to_space_haloed(field_in):
    blocks = lax.axis_size(("ta", "col"))
    rows = with_halo(field_in, (("row", 2),), 1)
    wide = jnp.pad(rows, ((0, 0), (0, 0), (0, 0), (1, 1)))
    block_cols = field_in.shape[3] // blocks
    windows = jnp.stack(
        [wide[..., j * block_cols : j * block_cols + block_cols + 2] for j in range(blocks)]
    )
    gathered = lax.all_to_all(windows, ("ta", "col"), split_axis=0, concat_axis=1, tiled=True)
    return gathered[0]


def to_time(field_in):
    return lax.all_to_all(field_in, ("ta", "col"), split_axis=0, concat_axis=3, tiled=True)


def time_mix(frames_in, time_taps):
    frame_count = frames_in.shape[0]
    padded = jnp.pad(frames_in, ((2, 2), (0, 0), (0, 0), (0, 0)))
    summed = jnp.zeros(frames_in.shape, jnp.float32)
    for tap_index in range(5):
        summed = summed + time_taps[None, :, tap_index, None, None] * padded[
            tap_index : tap_index + frame_count
        ].astype(jnp.float32)
    return summed


def gelu_exact(values_in):
    return jax.nn.gelu(values_in, approximate=False)


def shift_table(dispersion, width_keep, width_wide):
    source_col = lax.broadcasted_iota(jnp.int32, (1, width_keep, width_wide), 1)
    target_col = lax.broadcasted_iota(jnp.int32, (1, width_keep, width_wide), 2)
    return (target_col == source_col + dispersion[:, None, None]).astype(jnp.float32)


def disperse(masked, table):
    return jnp.einsum(
        "fbqw,bwv->fqv",
        masked,
        table,
        precision=lax.Precision.HIGHEST,
        preferred_element_type=jnp.float32,
    )


def undisperse(field_in, table):
    return jnp.einsum(
        "fqv,bwv->fbqw",
        field_in,
        table,
        precision=lax.Precision.HIGHEST,
        preferred_element_type=jnp.float32,
    )


def on_device(
    features,
    conv_weight,
    time_weight,
    band_out,
    band_input_weight,
    measured,
    aperture,
    dispersion,
    update_cot,
):
    feature_halo = with_halo(features, (("row", 2), (("ta", "col"), 3)), 2)
    pre_act_wide = valid_conv(feature_halo, conv_weight)
    pre_act = pre_act_wide[:, :, 1:-1, 1:-1]
    hidden_state = (features.astype(jnp.float32) + gelu_exact(pre_act)).astype(jnp.bfloat16)
    temporal = to_time(time_mix(hidden_state, time_weight).astype(jnp.bfloat16))
    width_keep = aperture.shape[-1]
    width_wide = measured.shape[-1]
    table = shift_table(dispersion, width_keep, width_wide)
    mask_float = aperture.astype(jnp.float32)[:, None]
    band_vals = jnp.einsum("fcqw,cb->fbqw", temporal, band_out, preferred_element_type=jnp.float32)
    masked_band_sum = disperse(band_vals * mask_float, table)
    residual_error = measured - masked_band_sum
    back_proj = (undisperse(residual_error, table) * mask_float).astype(jnp.bfloat16)
    updated = (
        temporal.astype(jnp.float32)
        + jnp.einsum(
            "fbqw,bc->fcqw", back_proj, band_input_weight, preferred_element_type=jnp.float32
        )
    ).astype(jnp.bfloat16)
    band_cot = jnp.einsum(
        "fcqw,bc->fbqw", update_cot, band_input_weight, preferred_element_type=jnp.float32
    )
    resid_grad = disperse(band_cot * mask_float, table)
    band_grad = (-(undisperse(resid_grad, table) * mask_float)).astype(jnp.bfloat16)
    cot_temporal = (
        update_cot.astype(jnp.float32)
        + jnp.einsum("fbqw,cb->fcqw", band_grad, band_out, preferred_element_type=jnp.float32)
    ).astype(jnp.bfloat16)
    flipped = time_weight[:, ::-1]
    cot_hidden_wide = time_mix(to_space_haloed(cot_temporal), flipped).astype(jnp.bfloat16)
    pullback = jax.vjp(gelu_exact, pre_act_wide)[1]
    gate_grad_wide = pullback(cot_hidden_wide.astype(jnp.float32))[0].astype(jnp.bfloat16)
    kernel_flip = jnp.transpose(conv_weight[::-1, ::-1], (0, 1, 3, 2))
    cot_hidden = cot_hidden_wide[:, :, 1:-1, 1:-1]
    features_grad = (
        cot_hidden.astype(jnp.float32) + valid_conv(gate_grad_wide, kernel_flip)
    ).astype(jnp.bfloat16)
    return (updated, features_grad)


def solution(mesh):
    return jax.shard_map(
        on_device,
        mesh=mesh,
        in_specs=(
            P(None, None, "row", ("ta", "col")),
            P(),
            P(),
            P(),
            P(),
            P(("ta", "col"), "row", None),
            P(("ta", "col"), "row", None),
            P(),
            P(("ta", "col"), None, "row", None),
        ),
        out_specs=(P(("ta", "col"), None, "row", None), P(None, None, "row", ("ta", "col"))),
        check_vma=False,
    )
```

```python
import jax
import jax.numpy as jnp
from jax import lax
from jax.sharding import PartitionSpec as P


def with_halo(array, sides, width):
    for axis, dim in sides:
        devices, length = (lax.axis_size(axis), array.shape[dim])
        up = [(i, (i + 1) % devices) for i in range(devices - 1)]
        down = [(j, i) for i, j in up]
        last = lax.slice_in_dim(array, length - width, length, axis=dim)
        initial = lax.slice_in_dim(array, 0, width, axis=dim)
        before = lax.ppermute(last, axis, up)
        after = lax.ppermute(initial, axis, down)
        array = jnp.concatenate([before, array, after], axis=dim)
    return array


def valid_conv(padded, kernel):
    return lax.conv_general_dilated(
        padded,
        kernel,
        window_strides=(1, 1),
        padding="VALID",
        dimension_numbers=("NCHW", "HWIO", "NCHW"),
        preferred_element_type=jnp.float32,
    )


def to_space_haloed(field_in):
    blocks = lax.axis_size(("ta", "col"))
    rows = with_halo(field_in, (("row", 2),), 1)
    lead = rows.shape[:3]
    split = rows.reshape(lead + (blocks, rows.shape[3] // blocks))
    left = jnp.pad(split[..., :-1, -1:], ((0, 0),) * 3 + ((1, 0), (0, 0)))
    right = jnp.pad(split[..., 1:, :1], ((0, 0),) * 3 + ((0, 1), (0, 0)))
    windows = jnp.moveaxis(jnp.concatenate([left, split, right], axis=-1), 3, 0)
    gathered = lax.all_to_all(windows, ("ta", "col"), split_axis=0, concat_axis=1, tiled=True)
    return gathered[0]


def to_time(field_in):
    return lax.all_to_all(field_in, ("ta", "col"), split_axis=0, concat_axis=3, tiled=True)


def time_mix(frames_in, time_taps):
    frame_count = frames_in.shape[0]
    padded = jnp.pad(frames_in, ((2, 2), (0, 0), (0, 0), (0, 0)))
    summed = jnp.zeros(frames_in.shape, jnp.float32)
    for tap_index in range(5):
        summed = summed + time_taps[None, :, tap_index, None, None] * padded[
            tap_index : tap_index + frame_count
        ].astype(jnp.float32)
    return summed


def gelu_exact(values_in):
    return jax.nn.gelu(values_in, approximate=False)


def shift_table(dispersion, width_keep, width_wide):
    source_col = lax.broadcasted_iota(jnp.int32, (1, width_keep, width_wide), 1)
    target_col = lax.broadcasted_iota(jnp.int32, (1, width_keep, width_wide), 2)
    return (target_col == source_col + dispersion[:, None, None]).astype(jnp.float32)


def disperse(masked, table):
    return jnp.einsum(
        "fbqw,bwv->fqv",
        masked,
        table,
        precision=lax.Precision.HIGHEST,
        preferred_element_type=jnp.float32,
    )


def undisperse(field_in, table):
    return jnp.einsum(
        "fqv,bwv->fbqw",
        field_in,
        table,
        precision=lax.Precision.HIGHEST,
        preferred_element_type=jnp.float32,
    )


def on_device(
    features,
    conv_weight,
    time_weight,
    band_out,
    band_input_weight,
    measured,
    aperture,
    dispersion,
    update_cot,
):
    feature_halo = with_halo(features, (("row", 2), (("ta", "col"), 3)), 2)
    pre_act_wide = valid_conv(feature_halo, conv_weight)
    gelu_wide, pullback = jax.vjp(gelu_exact, pre_act_wide)
    slope_wide = pullback(jnp.ones_like(pre_act_wide))[0]
    hidden_state = (
        features.astype(jnp.float32) + gelu_wide[:, :, 1:-1, 1:-1]
    ).astype(jnp.bfloat16)
    temporal = to_time(time_mix(hidden_state, time_weight).astype(jnp.bfloat16))
    width_keep = aperture.shape[-1]
    width_wide = measured.shape[-1]
    table = shift_table(dispersion, width_keep, width_wide)
    mask_float = aperture.astype(jnp.float32)[:, None]
    band_vals = jnp.einsum("fcqw,cb->fbqw", temporal, band_out, preferred_element_type=jnp.float32)
    masked_band_sum = disperse(band_vals * mask_float, table)
    residual_error = measured - masked_band_sum
    back_proj = (undisperse(residual_error, table) * mask_float).astype(jnp.bfloat16)
    updated = (
        temporal.astype(jnp.float32)
        + jnp.einsum(
            "fbqw,bc->fcqw", back_proj, band_input_weight, preferred_element_type=jnp.float32
        )
    ).astype(jnp.bfloat16)
    band_cot = jnp.einsum(
        "fcqw,bc->fbqw", update_cot, band_input_weight, preferred_element_type=jnp.float32
    )
    resid_grad = disperse(band_cot * mask_float, table)
    band_grad = (-(undisperse(resid_grad, table) * mask_float)).astype(jnp.bfloat16)
    cot_temporal = (
        update_cot.astype(jnp.float32)
        + jnp.einsum("fbqw,cb->fcqw", band_grad, band_out, preferred_element_type=jnp.float32)
    ).astype(jnp.bfloat16)
    flipped = time_weight[:, ::-1]
    cot_hidden_wide = time_mix(to_space_haloed(cot_temporal), flipped).astype(jnp.bfloat16)
    gate_grad_wide = lax.optimization_barrier(
        (slope_wide * cot_hidden_wide.astype(jnp.float32)).astype(jnp.bfloat16)
    )
    kernel_flip = jnp.transpose(conv_weight[::-1, ::-1], (0, 1, 3, 2))
    cot_hidden = cot_hidden_wide[:, :, 1:-1, 1:-1]
    features_grad = (
        cot_hidden.astype(jnp.float32) + valid_conv(gate_grad_wide, kernel_flip)
    ).astype(jnp.bfloat16)
    return (updated, features_grad)


def solution(mesh):
    return jax.shard_map(
        on_device,
        mesh=mesh,
        in_specs=(
            P(None, None, "row", ("ta", "col")),
            P(),
            P(),
            P(),
            P(),
            P(("ta", "col"), "row", None),
            P(("ta", "col"), "row", None),
            P(),
            P(("ta", "col"), None, "row", None),
        ),
        out_specs=(P(("ta", "col"), None, "row", None), P(None, None, "row", ("ta", "col"))),
        check_vma=False,
    )
```

```python
import jax
import jax.numpy as jnp
from jax import lax
from jax.sharding import PartitionSpec as P


def with_halo(array, sides, width):
    for axis, dim in sides:
        devices, length = (lax.axis_size(axis), array.shape[dim])
        up = [(i, (i + 1) % devices) for i in range(devices - 1)]
        down = [(j, i) for i, j in up]
        last = lax.slice_in_dim(array, length - width, length, axis=dim)
        initial = lax.slice_in_dim(array, 0, width, axis=dim)
        before = lax.ppermute(last, axis, up)
        after = lax.ppermute(initial, axis, down)
        array = jnp.concatenate([before, array, after], axis=dim)
    return array


def tile_halo(array, width):
    rows = lax.axis_size("row")
    ta_size, col_size = lax.axis_size("ta"), lax.axis_size("col")
    cols = ta_size * col_size

    def index(r, c):
        return (c // col_size) * rows * col_size + r * col_size + c % col_size

    def shifted(part, dr, dc):
        pairs = [
            (index(r, c), index(r + dr, c + dc))
            for r in range(rows)
            for c in range(cols)
            if 0 <= r + dr < rows and 0 <= c + dc < cols
        ]
        return lax.ppermute(part, ("ta", "row", "col"), pairs)

    top, bottom = array[:, :, :width], array[:, :, -width:]
    above = shifted(bottom, 1, 0)
    below = shifted(top, -1, 0)
    left = shifted(array[..., -width:], 0, 1)
    right = shifted(array[..., :width], 0, -1)
    above_left = shifted(bottom[..., -width:], 1, 1)
    above_right = shifted(bottom[..., :width], 1, -1)
    below_left = shifted(top[..., -width:], -1, 1)
    below_right = shifted(top[..., :width], -1, -1)
    upper = jnp.concatenate([above_left, above, above_right], axis=3)
    middle = jnp.concatenate([left, array, right], axis=3)
    lower = jnp.concatenate([below_left, below, below_right], axis=3)
    return jnp.concatenate([upper, middle, lower], axis=2)


def valid_conv(padded, kernel):
    return lax.conv_general_dilated(
        padded,
        kernel,
        window_strides=(1, 1),
        padding="VALID",
        dimension_numbers=("NCHW", "HWIO", "NCHW"),
        preferred_element_type=jnp.float32,
    )


def to_space_haloed(rows):
    blocks = lax.axis_size(("ta", "col"))
    lead = rows.shape[:3]
    split = rows.reshape(lead + (blocks, rows.shape[3] // blocks))
    left = jnp.pad(split[..., :-1, -1:], ((0, 0),) * 3 + ((1, 0), (0, 0)))
    right = jnp.pad(split[..., 1:, :1], ((0, 0),) * 3 + ((0, 1), (0, 0)))
    windows = jnp.moveaxis(jnp.concatenate([left, split, right], axis=-1), 3, 0)
    gathered = lax.all_to_all(windows, ("ta", "col"), split_axis=0, concat_axis=1, tiled=True)
    return gathered[0]


def to_time(field_in):
    return lax.all_to_all(field_in, ("ta", "col"), split_axis=0, concat_axis=3, tiled=True)


def time_mix(frames_in, time_taps):
    frame_count = frames_in.shape[0]
    padded = jnp.pad(frames_in, ((2, 2), (0, 0), (0, 0), (0, 0)))
    summed = jnp.zeros(frames_in.shape, jnp.float32)
    for tap_index in range(5):
        summed = summed + time_taps[None, :, tap_index, None, None] * padded[
            tap_index : tap_index + frame_count
        ].astype(jnp.float32)
    return summed


def gelu_exact(values_in):
    return jax.nn.gelu(values_in, approximate=False)


def shift_table(dispersion, width_keep, width_wide):
    source_col = lax.broadcasted_iota(jnp.int32, (1, width_keep, width_wide), 1)
    target_col = lax.broadcasted_iota(jnp.int32, (1, width_keep, width_wide), 2)
    return (target_col == source_col + dispersion[:, None, None]).astype(jnp.float32)


def disperse(masked, table):
    return jnp.einsum(
        "fbqw,bwv->fqv",
        masked,
        table,
        precision=lax.Precision.HIGHEST,
        preferred_element_type=jnp.float32,
    )


def undisperse(field_in, table):
    return jnp.einsum(
        "fqv,bwv->fbqw",
        field_in,
        table,
        precision=lax.Precision.HIGHEST,
        preferred_element_type=jnp.float32,
    )


def on_device(
    features,
    conv_weight,
    time_weight,
    band_out,
    band_input_weight,
    measured,
    aperture,
    dispersion,
    update_cot,
):
    feature_halo = tile_halo(features, 2)
    channels = update_cot.shape[1]
    cot_rows = with_halo(
        jnp.concatenate([update_cot, aperture.astype(jnp.bfloat16)[:, None]], axis=1),
        (("row", 2),),
        1,
    )
    feature_halo, cot_rows = lax.optimization_barrier((feature_halo, cot_rows))
    pre_act_wide = valid_conv(feature_halo, conv_weight)
    gelu_wide, pullback = jax.vjp(gelu_exact, pre_act_wide)
    slope_wide = pullback(jnp.ones_like(pre_act_wide))[0]
    hidden_state = (
        features.astype(jnp.float32) + gelu_wide[:, :, 1:-1, 1:-1]
    ).astype(jnp.bfloat16)
    temporal = to_time(time_mix(hidden_state, time_weight).astype(jnp.bfloat16))
    width_keep = aperture.shape[-1]
    width_wide = measured.shape[-1]
    table = shift_table(dispersion, width_keep, width_wide)
    mask_float = aperture.astype(jnp.float32)[:, None]
    band_vals = jnp.einsum("fcqw,cb->fbqw", temporal, band_out, preferred_element_type=jnp.float32)
    masked_band_sum = disperse(band_vals * mask_float, table)
    residual_error = measured - masked_band_sum
    back_proj = (undisperse(residual_error, table) * mask_float).astype(jnp.bfloat16)
    updated = (
        temporal.astype(jnp.float32)
        + jnp.einsum(
            "fbqw,bc->fcqw", back_proj, band_input_weight, preferred_element_type=jnp.float32
        )
    ).astype(jnp.bfloat16)
    update_cot_rows = cot_rows[:, :channels]
    mask_rows = cot_rows[:, channels:].astype(jnp.float32)
    band_cot = jnp.einsum(
        "fcqw,bc->fbqw", update_cot_rows, band_input_weight, preferred_element_type=jnp.float32
    )
    resid_grad = disperse(band_cot * mask_rows, table)
    band_grad = (-(undisperse(resid_grad, table) * mask_rows)).astype(jnp.bfloat16)
    cot_temporal_rows = (
        update_cot_rows.astype(jnp.float32)
        + jnp.einsum("fbqw,cb->fcqw", band_grad, band_out, preferred_element_type=jnp.float32)
    ).astype(jnp.bfloat16)
    flipped = time_weight[:, ::-1]
    cot_hidden_wide = time_mix(to_space_haloed(cot_temporal_rows), flipped).astype(jnp.bfloat16)
    gate_grad_wide = lax.optimization_barrier(
        (slope_wide * cot_hidden_wide.astype(jnp.float32)).astype(jnp.bfloat16)
    )
    kernel_flip = jnp.transpose(conv_weight[::-1, ::-1], (0, 1, 3, 2))
    cot_hidden = cot_hidden_wide[:, :, 1:-1, 1:-1]
    features_grad = (
        cot_hidden.astype(jnp.float32) + valid_conv(gate_grad_wide, kernel_flip)
    ).astype(jnp.bfloat16)
    return (updated, features_grad)


def solution(mesh):
    return jax.shard_map(
        on_device,
        mesh=mesh,
        in_specs=(
            P(None, None, "row", ("ta", "col")),
            P(),
            P(),
            P(),
            P(),
            P(("ta", "col"), "row", None),
            P(("ta", "col"), "row", None),
            P(),
            P(("ta", "col"), None, "row", None),
        ),
        out_specs=(P(("ta", "col"), None, "row", None), P(None, None, "row", ("ta", "col"))),
        check_vma=False,
    )
```

```python
import jax
import jax.numpy as jnp
from jax import lax
from jax.sharding import PartitionSpec as P


def with_halo(array, sides, width):
    for axis, dim in sides:
        devices, length = (lax.axis_size(axis), array.shape[dim])
        up = [(i, (i + 1) % devices) for i in range(devices - 1)]
        down = [(j, i) for i, j in up]
        last = lax.slice_in_dim(array, length - width, length, axis=dim)
        initial = lax.slice_in_dim(array, 0, width, axis=dim)
        before = lax.ppermute(last, axis, up)
        after = lax.ppermute(initial, axis, down)
        array = jnp.concatenate([before, array, after], axis=dim)
    return array


def tile_halo(array, width):
    rows = lax.axis_size("row")
    ta_size, col_size = lax.axis_size("ta"), lax.axis_size("col")
    cols = ta_size * col_size

    def index(r, c):
        return (c // col_size) * rows * col_size + r * col_size + c % col_size

    def shifted(part, dr, dc):
        pairs = [
            (index(r, c), index(r + dr, c + dc))
            for r in range(rows)
            for c in range(cols)
            if 0 <= r + dr < rows and 0 <= c + dc < cols
        ]
        return lax.ppermute(part, ("ta", "row", "col"), pairs)

    top, bottom = array[:, :, :width], array[:, :, -width:]
    above = shifted(bottom, 1, 0)
    below = shifted(top, -1, 0)
    left = shifted(array[..., -width:], 0, 1)
    right = shifted(array[..., :width], 0, -1)
    above_left = shifted(bottom[..., -width:], 1, 1)
    above_right = shifted(bottom[..., :width], 1, -1)
    below_left = shifted(top[..., -width:], -1, 1)
    below_right = shifted(top[..., :width], -1, -1)
    upper = jnp.concatenate([above_left, above, above_right], axis=3)
    middle = jnp.concatenate([left, array, right], axis=3)
    lower = jnp.concatenate([below_left, below, below_right], axis=3)
    return jnp.concatenate([upper, middle, lower], axis=2)


def valid_conv(padded, kernel):
    return lax.conv_general_dilated(
        padded,
        kernel,
        window_strides=(1, 1),
        padding="VALID",
        dimension_numbers=("NCHW", "HWIO", "NCHW"),
        preferred_element_type=jnp.float32,
    )


def to_space_haloed(rows):
    blocks = lax.axis_size(("ta", "col"))
    lead = rows.shape[:3]
    split = rows.reshape(lead + (blocks, rows.shape[3] // blocks))
    left = jnp.pad(split[..., :-1, -1:], ((0, 0),) * 3 + ((1, 0), (0, 0)))
    right = jnp.pad(split[..., 1:, :1], ((0, 0),) * 3 + ((0, 1), (0, 0)))
    windows = jnp.moveaxis(jnp.concatenate([left, split, right], axis=-1), 3, 0)
    gathered = lax.all_to_all(windows, ("ta", "col"), split_axis=0, concat_axis=1, tiled=True)
    return gathered[0]


def to_time(field_in):
    return lax.all_to_all(field_in, ("ta", "col"), split_axis=0, concat_axis=3, tiled=True)


def time_mix(frames_in, time_taps):
    frame_count = frames_in.shape[0]
    padded = jnp.pad(frames_in, ((2, 2), (0, 0), (0, 0), (0, 0)))
    summed = jnp.zeros(frames_in.shape, jnp.float32)
    for tap_index in range(5):
        summed = summed + time_taps[None, :, tap_index, None, None] * padded[
            tap_index : tap_index + frame_count
        ].astype(jnp.float32)
    return summed


def gelu_exact(values_in):
    return jax.nn.gelu(values_in, approximate=False)


def shift_table(dispersion, width_keep, width_wide):
    source_col = lax.broadcasted_iota(jnp.int32, (1, width_keep, width_wide), 1)
    target_col = lax.broadcasted_iota(jnp.int32, (1, width_keep, width_wide), 2)
    return (target_col == source_col + dispersion[:, None, None]).astype(jnp.float32)


def disperse(masked, table):
    return jnp.einsum(
        "fbqw,bwv->fqv",
        masked,
        table,
        precision=lax.Precision.HIGHEST,
        preferred_element_type=jnp.float32,
    )


def undisperse(field_in, table):
    return jnp.einsum(
        "fqv,bwv->fbqw",
        field_in,
        table,
        precision=lax.Precision.HIGHEST,
        preferred_element_type=jnp.float32,
    )


def on_device(
    features,
    conv_weight,
    time_weight,
    band_out,
    band_input_weight,
    measured,
    aperture,
    dispersion,
    update_cot,
):
    channels = update_cot.shape[1]
    cot_source = jnp.concatenate([update_cot, aperture.astype(jnp.bfloat16)[:, None]], axis=1)
    rows = lax.axis_size("row")
    down = [(i, i + 1) for i in range(rows - 1)]
    up = [(j, i) for i, j in down]
    feature_edge = features[:, :, :2].shape
    cot_edge = cot_source[:, :, :1].shape
    cut = features[:, :, :2].size

    def packed(feature_part, cot_part):
        return jnp.concatenate([feature_part.reshape(-1), cot_part.reshape(-1)])

    from_above = lax.ppermute(packed(features[:, :, -2:], cot_source[:, :, -1:]), "row", down)
    from_below = lax.ppermute(packed(features[:, :, :2], cot_source[:, :, :1]), "row", up)
    feature_rows = jnp.concatenate(
        [
            from_above[:cut].reshape(feature_edge),
            features,
            from_below[:cut].reshape(feature_edge),
        ],
        axis=2,
    )
    cot_rows = jnp.concatenate(
        [from_above[cut:].reshape(cot_edge), cot_source, from_below[cut:].reshape(cot_edge)],
        axis=2,
    )
    feature_halo = with_halo(feature_rows, ((("ta", "col"), 3),), 2)
    pre_act_wide = valid_conv(feature_halo, conv_weight)
    gelu_wide, pullback = jax.vjp(gelu_exact, pre_act_wide)
    slope_wide = pullback(jnp.ones_like(pre_act_wide))[0]
    hidden_state = (
        features.astype(jnp.float32) + gelu_wide[:, :, 1:-1, 1:-1]
    ).astype(jnp.bfloat16)
    temporal = to_time(time_mix(hidden_state, time_weight).astype(jnp.bfloat16))
    width_keep = aperture.shape[-1]
    width_wide = measured.shape[-1]
    table = shift_table(dispersion, width_keep, width_wide)
    mask_float = aperture.astype(jnp.float32)[:, None]
    band_vals = jnp.einsum("fcqw,cb->fbqw", temporal, band_out, preferred_element_type=jnp.float32)
    masked_band_sum = disperse(band_vals * mask_float, table)
    residual_error = measured - masked_band_sum
    back_proj = (undisperse(residual_error, table) * mask_float).astype(jnp.bfloat16)
    updated = (
        temporal.astype(jnp.float32)
        + jnp.einsum(
            "fbqw,bc->fcqw", back_proj, band_input_weight, preferred_element_type=jnp.float32
        )
    ).astype(jnp.bfloat16)
    update_cot_rows = cot_rows[:, :channels]
    mask_rows = cot_rows[:, channels:].astype(jnp.float32)
    band_cot = jnp.einsum(
        "fcqw,bc->fbqw", update_cot_rows, band_input_weight, preferred_element_type=jnp.float32
    )
    resid_grad = disperse(band_cot * mask_rows, table)
    band_grad = (-(undisperse(resid_grad, table) * mask_rows)).astype(jnp.bfloat16)
    cot_temporal_rows = (
        update_cot_rows.astype(jnp.float32)
        + jnp.einsum("fbqw,cb->fcqw", band_grad, band_out, preferred_element_type=jnp.float32)
    ).astype(jnp.bfloat16)
    flipped = time_weight[:, ::-1]
    cot_hidden_wide = time_mix(to_space_haloed(cot_temporal_rows), flipped).astype(jnp.bfloat16)
    gate_grad_wide = lax.optimization_barrier(
        (slope_wide * cot_hidden_wide.astype(jnp.float32)).astype(jnp.bfloat16)
    )
    kernel_flip = jnp.transpose(conv_weight[::-1, ::-1], (0, 1, 3, 2))
    cot_hidden = cot_hidden_wide[:, :, 1:-1, 1:-1]
    features_grad = (
        cot_hidden.astype(jnp.float32) + valid_conv(gate_grad_wide, kernel_flip)
    ).astype(jnp.bfloat16)
    return (updated, features_grad)


def solution(mesh):
    return jax.shard_map(
        on_device,
        mesh=mesh,
        in_specs=(
            P(None, None, "row", ("ta", "col")),
            P(),
            P(),
            P(),
            P(),
            P(("ta", "col"), "row", None),
            P(("ta", "col"), "row", None),
            P(),
            P(("ta", "col"), None, "row", None),
        ),
        out_specs=(P(("ta", "col"), None, "row", None), P(None, None, "row", ("ta", "col"))),
        check_vma=False,
    )
```

```python
import jax
import jax.numpy as jnp
from jax import lax
from jax.sharding import PartitionSpec as P


def with_halo(array, sides, width):
    for axis, dim in sides:
        devices, length = (lax.axis_size(axis), array.shape[dim])
        up = [(i, (i + 1) % devices) for i in range(devices - 1)]
        down = [(j, i) for i, j in up]
        last = lax.slice_in_dim(array, length - width, length, axis=dim)
        initial = lax.slice_in_dim(array, 0, width, axis=dim)
        before = lax.ppermute(last, axis, up)
        after = lax.ppermute(initial, axis, down)
        array = jnp.concatenate([before, array, after], axis=dim)
    return array


def spatial_conv(field_in, kernel):
    padded = with_halo(field_in, (("row", 2), (("ta", "col"), 3)), 1)
    return lax.conv_general_dilated(
        padded,
        kernel,
        window_strides=(1, 1),
        padding="VALID",
        dimension_numbers=("NCHW", "HWIO", "NCHW"),
        preferred_element_type=jnp.float32,
    )


def to_time(field_in):
    return lax.all_to_all(field_in, ("ta", "col"), split_axis=0, concat_axis=3, tiled=True)


def to_space(field_in):
    return lax.all_to_all(field_in, ("ta", "col"), split_axis=3, concat_axis=0, tiled=True)


def time_mix(frames_in, time_taps):
    frame_count = frames_in.shape[0]
    padded = jnp.pad(frames_in, ((2, 2), (0, 0), (0, 0), (0, 0)))
    summed = jnp.zeros(frames_in.shape, jnp.float32)
    for tap_index in range(5):
        summed = summed + time_taps[None, :, tap_index, None, None] * padded[
            tap_index : tap_index + frame_count
        ].astype(jnp.float32)
    return summed


def gelu_exact(values_in):
    return jax.nn.gelu(values_in, approximate=False)


def shift_bits(dispersion, largest):
    bits = largest.bit_length()
    return [((dispersion >> k) & 1).astype(bool)[None, :, None, None] for k in range(bits)]


def disperse(masked, bits, width_wide):
    moved = jnp.pad(masked, ((0, 0),) * 3 + ((0, width_wide - masked.shape[-1]),))
    for k, bit in enumerate(bits):
        step = 1 << k
        later = jnp.pad(moved[..., :-step], ((0, 0),) * 3 + ((step, 0),))
        moved = jnp.where(bit, later, moved)
    return jnp.sum(moved, axis=1)


def undisperse(field_in, bits, width_keep):
    moved = jnp.broadcast_to(
        field_in[:, None], (field_in.shape[0], bits[0].shape[1]) + field_in.shape[1:]
    )
    for k, bit in enumerate(bits):
        step = 1 << k
        earlier = jnp.pad(moved[..., step:], ((0, 0),) * 3 + ((0, step),))
        moved = jnp.where(bit, earlier, moved)
    return moved[..., :width_keep]


def on_device(
    features,
    conv_weight,
    time_weight,
    band_out,
    band_input_weight,
    measured,
    aperture,
    dispersion,
    update_cot,
):
    pre_act = spatial_conv(features, conv_weight)
    hidden_state = (features.astype(jnp.float32) + gelu_exact(pre_act)).astype(jnp.bfloat16)
    temporal = to_time(time_mix(hidden_state, time_weight).astype(jnp.bfloat16))
    width_keep = aperture.shape[-1]
    width_wide = measured.shape[-1]
    bits = shift_bits(dispersion, width_wide - width_keep)
    mask_float = aperture.astype(jnp.float32)[:, None]
    band_vals = jnp.einsum("fcqw,cb->fbqw", temporal, band_out, preferred_element_type=jnp.float32)
    masked_band_sum = disperse(band_vals * mask_float, bits, width_wide)
    residual_error = measured - masked_band_sum
    back_proj = (undisperse(residual_error, bits, width_keep) * mask_float).astype(jnp.bfloat16)
    updated = (
        temporal.astype(jnp.float32)
        + jnp.einsum(
            "fbqw,bc->fcqw", back_proj, band_input_weight, preferred_element_type=jnp.float32
        )
    ).astype(jnp.bfloat16)
    band_cot = jnp.einsum(
        "fcqw,bc->fbqw", update_cot, band_input_weight, preferred_element_type=jnp.float32
    )
    resid_grad = disperse(band_cot * mask_float, bits, width_wide)
    band_grad = (-(undisperse(resid_grad, bits, width_keep) * mask_float)).astype(jnp.bfloat16)
    cot_temporal = (
        update_cot.astype(jnp.float32)
        + jnp.einsum("fbqw,cb->fcqw", band_grad, band_out, preferred_element_type=jnp.float32)
    ).astype(jnp.bfloat16)
    flipped = time_weight[:, ::-1]
    cot_hidden = time_mix(to_space(cot_temporal), flipped).astype(jnp.bfloat16)
    pullback = jax.vjp(gelu_exact, pre_act)[1]
    gate_grad = pullback(cot_hidden.astype(jnp.float32))[0].astype(jnp.bfloat16)
    kernel_flip = jnp.transpose(conv_weight[::-1, ::-1], (0, 1, 3, 2))
    features_grad = (cot_hidden.astype(jnp.float32) + spatial_conv(gate_grad, kernel_flip)).astype(
        jnp.bfloat16
    )
    return (updated, features_grad)


def solution(mesh):
    return jax.shard_map(
        on_device,
        mesh=mesh,
        in_specs=(
            P(None, None, "row", ("ta", "col")),
            P(),
            P(),
            P(),
            P(),
            P(("ta", "col"), "row", None),
            P(("ta", "col"), "row", None),
            P(),
            P(("ta", "col"), None, "row", None),
        ),
        out_specs=(P(("ta", "col"), None, "row", None), P(None, None, "row", ("ta", "col"))),
        check_vma=False,
    )
```

```python
import jax
import jax.numpy as jnp
from jax import lax
from jax.sharding import PartitionSpec as P


def with_halo(array, sides, width):
    for axis, dim in sides:
        devices, length = (lax.axis_size(axis), array.shape[dim])
        up = [(i, (i + 1) % devices) for i in range(devices - 1)]
        down = [(j, i) for i, j in up]
        last = lax.slice_in_dim(array, length - width, length, axis=dim)
        initial = lax.slice_in_dim(array, 0, width, axis=dim)
        before = lax.ppermute(last, axis, up)
        after = lax.ppermute(initial, axis, down)
        array = jnp.concatenate([before, array, after], axis=dim)
    return array


def spatial_conv(field_in, kernel):
    padded = with_halo(field_in, (("row", 2), (("ta", "col"), 3)), 1)
    return lax.conv_general_dilated(
        padded,
        kernel,
        window_strides=(1, 1),
        padding="VALID",
        dimension_numbers=("NCHW", "HWIO", "NCHW"),
        preferred_element_type=jnp.float32,
    )


def to_time(field_in):
    return lax.all_to_all(field_in, ("ta", "col"), split_axis=0, concat_axis=3, tiled=True)


def to_space(field_in):
    return lax.all_to_all(field_in, ("ta", "col"), split_axis=3, concat_axis=0, tiled=True)


def time_mix(frames_in, time_taps):
    frame_count = frames_in.shape[0]
    padded = jnp.pad(frames_in, ((2, 2), (0, 0), (0, 0), (0, 0)))
    summed = jnp.zeros(frames_in.shape, jnp.float32)
    for tap_index in range(5):
        summed = summed + time_taps[None, :, tap_index, None, None] * padded[
            tap_index : tap_index + frame_count
        ].astype(jnp.float32)
    return summed


def gelu_exact(values_in):
    return jax.nn.gelu(values_in, approximate=False)


def shift_bits(dispersion, largest):
    bits = largest.bit_length()
    return [((dispersion >> k) & 1).astype(bool)[None, :, None, None] for k in range(bits)]


def disperse(masked, bits, width_wide):
    moved = jnp.pad(masked, ((0, 0),) * 3 + ((0, width_wide - masked.shape[-1]),))
    for k, bit in enumerate(bits):
        step = 1 << k
        later = jnp.pad(moved[..., :-step], ((0, 0),) * 3 + ((step, 0),))
        moved = jnp.where(bit, later, moved)
    return jnp.sum(moved, axis=1)


def undisperse(field_in, bits, width_keep):
    moved = jnp.broadcast_to(
        field_in[:, None], (field_in.shape[0], bits[0].shape[1]) + field_in.shape[1:]
    )
    for k, bit in enumerate(bits):
        step = 1 << k
        earlier = jnp.pad(moved[..., step:], ((0, 0),) * 3 + ((0, step),))
        moved = jnp.where(bit, earlier, moved)
    return moved[..., :width_keep]


def on_device(
    features,
    conv_weight,
    time_weight,
    band_out,
    band_input_weight,
    measured,
    aperture,
    dispersion,
    update_cot,
):
    width_keep = aperture.shape[-1]
    width_wide = measured.shape[-1]
    bits = shift_bits(dispersion, width_wide - width_keep)
    mask_float = aperture.astype(jnp.float32)[:, None]
    band_cot = jnp.einsum(
        "fcqw,bc->fbqw", update_cot, band_input_weight, preferred_element_type=jnp.float32
    )
    resid_grad = disperse(band_cot * mask_float, bits, width_wide)
    band_grad = (-(undisperse(resid_grad, bits, width_keep) * mask_float)).astype(jnp.bfloat16)
    cot_temporal = (
        update_cot.astype(jnp.float32)
        + jnp.einsum("fbqw,cb->fcqw", band_grad, band_out, preferred_element_type=jnp.float32)
    ).astype(jnp.bfloat16)
    features, cot_temporal = lax.optimization_barrier((features, cot_temporal))
    pre_act = spatial_conv(features, conv_weight)
    hidden_state = (features.astype(jnp.float32) + gelu_exact(pre_act)).astype(jnp.bfloat16)
    temporal = to_time(time_mix(hidden_state, time_weight).astype(jnp.bfloat16))
    band_vals = jnp.einsum("fcqw,cb->fbqw", temporal, band_out, preferred_element_type=jnp.float32)
    masked_band_sum = disperse(band_vals * mask_float, bits, width_wide)
    residual_error = measured - masked_band_sum
    back_proj = (undisperse(residual_error, bits, width_keep) * mask_float).astype(jnp.bfloat16)
    updated = (
        temporal.astype(jnp.float32)
        + jnp.einsum(
            "fbqw,bc->fcqw", back_proj, band_input_weight, preferred_element_type=jnp.float32
        )
    ).astype(jnp.bfloat16)
    flipped = time_weight[:, ::-1]
    cot_hidden = time_mix(to_space(cot_temporal), flipped).astype(jnp.bfloat16)
    pullback = jax.vjp(gelu_exact, pre_act)[1]
    gate_grad = pullback(cot_hidden.astype(jnp.float32))[0].astype(jnp.bfloat16)
    kernel_flip = jnp.transpose(conv_weight[::-1, ::-1], (0, 1, 3, 2))
    features_grad = (cot_hidden.astype(jnp.float32) + spatial_conv(gate_grad, kernel_flip)).astype(
        jnp.bfloat16
    )
    return (updated, features_grad)


def solution(mesh):
    return jax.shard_map(
        on_device,
        mesh=mesh,
        in_specs=(
            P(None, None, "row", ("ta", "col")),
            P(),
            P(),
            P(),
            P(),
            P(("ta", "col"), "row", None),
            P(("ta", "col"), "row", None),
            P(),
            P(("ta", "col"), None, "row", None),
        ),
        out_specs=(P(("ta", "col"), None, "row", None), P(None, None, "row", ("ta", "col"))),
        check_vma=False,
    )
```

```python
import jax
import jax.numpy as jnp
from jax import lax
from jax.sharding import PartitionSpec as P


def with_halo(array, sides, width):
    for axis, dim in sides:
        devices, length = (lax.axis_size(axis), array.shape[dim])
        up = [(i, (i + 1) % devices) for i in range(devices - 1)]
        down = [(j, i) for i, j in up]
        last = lax.slice_in_dim(array, length - width, length, axis=dim)
        initial = lax.slice_in_dim(array, 0, width, axis=dim)
        before = lax.ppermute(last, axis, up)
        after = lax.ppermute(initial, axis, down)
        array = jnp.concatenate([before, array, after], axis=dim)
    return array


def row_halo(field_in):
    return with_halo(field_in, (("row", 2),), 1)


def halo_conv(rows, kernel):
    padded = with_halo(rows, ((("ta", "col"), 3),), 1)
    return lax.conv_general_dilated(
        padded,
        kernel,
        window_strides=(1, 1),
        padding="VALID",
        dimension_numbers=("NCHW", "HWIO", "NCHW"),
        preferred_element_type=jnp.float32,
    )


def to_time(field_in):
    return lax.all_to_all(field_in, ("ta", "col"), split_axis=0, concat_axis=3, tiled=True)


def to_space(field_in):
    return lax.all_to_all(field_in, ("ta", "col"), split_axis=3, concat_axis=0, tiled=True)


def time_mix(frames_in, time_taps):
    frame_count = frames_in.shape[0]
    padded = jnp.pad(frames_in, ((2, 2), (0, 0), (0, 0), (0, 0)))
    summed = jnp.zeros(frames_in.shape, jnp.float32)
    for tap_index in range(5):
        summed = summed + time_taps[None, :, tap_index, None, None] * padded[
            tap_index : tap_index + frame_count
        ].astype(jnp.float32)
    return summed


def gelu_exact(values_in):
    return jax.nn.gelu(values_in, approximate=False)


def shift_bits(dispersion, largest):
    bits = largest.bit_length()
    return [((dispersion >> k) & 1).astype(bool)[None, :, None, None] for k in range(bits)]


def disperse(masked, bits, width_wide):
    moved = jnp.pad(masked, ((0, 0),) * 3 + ((0, width_wide - masked.shape[-1]),))
    for k, bit in enumerate(bits):
        step = 1 << k
        later = jnp.pad(moved[..., :-step], ((0, 0),) * 3 + ((step, 0),))
        moved = jnp.where(bit, later, moved)
    return jnp.sum(moved, axis=1)


def undisperse(field_in, bits, width_keep):
    moved = jnp.broadcast_to(
        field_in[:, None], (field_in.shape[0], bits[0].shape[1]) + field_in.shape[1:]
    )
    for k, bit in enumerate(bits):
        step = 1 << k
        earlier = jnp.pad(moved[..., step:], ((0, 0),) * 3 + ((0, step),))
        moved = jnp.where(bit, earlier, moved)
    return moved[..., :width_keep]


def on_device(
    features,
    conv_weight,
    time_weight,
    band_out,
    band_input_weight,
    measured,
    aperture,
    dispersion,
    update_cot,
):
    width_keep = aperture.shape[-1]
    width_wide = measured.shape[-1]
    bits = shift_bits(dispersion, width_wide - width_keep)
    mask_float = aperture.astype(jnp.float32)[:, None]
    band_cot = jnp.einsum(
        "fcqw,bc->fbqw", update_cot, band_input_weight, preferred_element_type=jnp.float32
    )
    resid_grad = disperse(band_cot * mask_float, bits, width_wide)
    band_grad = (-(undisperse(resid_grad, bits, width_keep) * mask_float)).astype(jnp.bfloat16)
    cot_temporal = (
        update_cot.astype(jnp.float32)
        + jnp.einsum("fbqw,cb->fcqw", band_grad, band_out, preferred_element_type=jnp.float32)
    ).astype(jnp.bfloat16)
    feature_rows = row_halo(features)
    feature_rows, cot_temporal = lax.optimization_barrier((feature_rows, cot_temporal))
    pre_act = halo_conv(feature_rows, conv_weight)
    hidden_state = (features.astype(jnp.float32) + gelu_exact(pre_act)).astype(jnp.bfloat16)
    temporal = to_time(time_mix(hidden_state, time_weight).astype(jnp.bfloat16))
    band_vals = jnp.einsum("fcqw,cb->fbqw", temporal, band_out, preferred_element_type=jnp.float32)
    masked_band_sum = disperse(band_vals * mask_float, bits, width_wide)
    residual_error = measured - masked_band_sum
    back_proj = (undisperse(residual_error, bits, width_keep) * mask_float).astype(jnp.bfloat16)
    updated = (
        temporal.astype(jnp.float32)
        + jnp.einsum(
            "fbqw,bc->fcqw", back_proj, band_input_weight, preferred_element_type=jnp.float32
        )
    ).astype(jnp.bfloat16)
    flipped = time_weight[:, ::-1]
    cot_hidden = time_mix(to_space(cot_temporal), flipped).astype(jnp.bfloat16)
    pullback = jax.vjp(gelu_exact, pre_act)[1]
    gate_grad = pullback(cot_hidden.astype(jnp.float32))[0].astype(jnp.bfloat16)
    kernel_flip = jnp.transpose(conv_weight[::-1, ::-1], (0, 1, 3, 2))
    gate_rows = row_halo(gate_grad)
    gate_rows, updated = lax.optimization_barrier((gate_rows, updated))
    features_grad = (cot_hidden.astype(jnp.float32) + halo_conv(gate_rows, kernel_flip)).astype(
        jnp.bfloat16
    )
    return (updated, features_grad)


def solution(mesh):
    return jax.shard_map(
        on_device,
        mesh=mesh,
        in_specs=(
            P(None, None, "row", ("ta", "col")),
            P(),
            P(),
            P(),
            P(),
            P(("ta", "col"), "row", None),
            P(("ta", "col"), "row", None),
            P(),
            P(("ta", "col"), None, "row", None),
        ),
        out_specs=(P(("ta", "col"), None, "row", None), P(None, None, "row", ("ta", "col"))),
        check_vma=False,
    )
```

```python
import jax
import jax.numpy as jnp
from jax import lax
from jax.sharding import PartitionSpec as P


def with_halo(array, sides, width):
    for axis, dim in sides:
        devices, length = (lax.axis_size(axis), array.shape[dim])
        up = [(i, (i + 1) % devices) for i in range(devices - 1)]
        down = [(j, i) for i, j in up]
        last = lax.slice_in_dim(array, length - width, length, axis=dim)
        initial = lax.slice_in_dim(array, 0, width, axis=dim)
        before = lax.ppermute(last, axis, up)
        after = lax.ppermute(initial, axis, down)
        array = jnp.concatenate([before, array, after], axis=dim)
    return array


def row_halo(field_in):
    return with_halo(field_in, (("row", 2),), 1)


def halo_conv(rows, kernel):
    padded = with_halo(rows, ((("ta", "col"), 3),), 1)
    return lax.conv_general_dilated(
        padded,
        kernel,
        window_strides=(1, 1),
        padding="VALID",
        dimension_numbers=("NCHW", "HWIO", "NCHW"),
        preferred_element_type=jnp.float32,
    )


def spatial_conv(field_in, kernel):
    return halo_conv(row_halo(field_in), kernel)


def to_time(field_in):
    return lax.all_to_all(field_in, ("ta", "col"), split_axis=0, concat_axis=3, tiled=True)


def to_space(field_in):
    return lax.all_to_all(field_in, ("ta", "col"), split_axis=3, concat_axis=0, tiled=True)


def time_mix(frames_in, time_taps):
    frame_count = frames_in.shape[0]
    padded = jnp.pad(frames_in, ((2, 2), (0, 0), (0, 0), (0, 0)))
    summed = jnp.zeros(frames_in.shape, jnp.float32)
    for tap_index in range(5):
        summed = summed + time_taps[None, :, tap_index, None, None] * padded[
            tap_index : tap_index + frame_count
        ].astype(jnp.float32)
    return summed


def gelu_exact(values_in):
    return jax.nn.gelu(values_in, approximate=False)


def shift_bits(dispersion, largest):
    bits = largest.bit_length()
    return [((dispersion >> k) & 1).astype(bool)[None, :, None, None] for k in range(bits)]


def disperse(masked, bits, width_wide):
    moved = jnp.pad(masked, ((0, 0),) * 3 + ((0, width_wide - masked.shape[-1]),))
    for k, bit in enumerate(bits):
        step = 1 << k
        later = jnp.pad(moved[..., :-step], ((0, 0),) * 3 + ((step, 0),))
        moved = jnp.where(bit, later, moved)
    return jnp.sum(moved, axis=1)


def undisperse(field_in, bits, width_keep):
    moved = jnp.broadcast_to(
        field_in[:, None], (field_in.shape[0], bits[0].shape[1]) + field_in.shape[1:]
    )
    for k, bit in enumerate(bits):
        step = 1 << k
        earlier = jnp.pad(moved[..., step:], ((0, 0),) * 3 + ((0, step),))
        moved = jnp.where(bit, earlier, moved)
    return moved[..., :width_keep]


def on_device(
    features,
    conv_weight,
    time_weight,
    band_out,
    band_input_weight,
    measured,
    aperture,
    dispersion,
    update_cot,
):
    width_keep = aperture.shape[-1]
    width_wide = measured.shape[-1]
    bits = shift_bits(dispersion, width_wide - width_keep)
    mask_float = aperture.astype(jnp.float32)[:, None]
    band_cot = jnp.einsum(
        "fcqw,bc->fbqw", update_cot, band_input_weight, preferred_element_type=jnp.float32
    )
    resid_grad = disperse(band_cot * mask_float, bits, width_wide)
    band_grad = (-(undisperse(resid_grad, bits, width_keep) * mask_float)).astype(jnp.bfloat16)
    cot_temporal = (
        update_cot.astype(jnp.float32)
        + jnp.einsum("fbqw,cb->fcqw", band_grad, band_out, preferred_element_type=jnp.float32)
    ).astype(jnp.bfloat16)
    feature_rows = row_halo(features)
    feature_rows, cot_temporal = lax.optimization_barrier((feature_rows, cot_temporal))
    pre_act = halo_conv(feature_rows, conv_weight)
    gelu_value, pullback = jax.vjp(gelu_exact, pre_act)
    slope = pullback(jnp.ones_like(pre_act))[0]
    hidden_state = (features.astype(jnp.float32) + gelu_value).astype(jnp.bfloat16)
    temporal = to_time(time_mix(hidden_state, time_weight).astype(jnp.bfloat16))
    band_vals = jnp.einsum("fcqw,cb->fbqw", temporal, band_out, preferred_element_type=jnp.float32)
    masked_band_sum = disperse(band_vals * mask_float, bits, width_wide)
    residual_error = measured - masked_band_sum
    back_proj = (undisperse(residual_error, bits, width_keep) * mask_float).astype(jnp.bfloat16)
    updated = (
        temporal.astype(jnp.float32)
        + jnp.einsum(
            "fbqw,bc->fcqw", back_proj, band_input_weight, preferred_element_type=jnp.float32
        )
    ).astype(jnp.bfloat16)
    flipped = time_weight[:, ::-1]
    cot_hidden = time_mix(to_space(cot_temporal), flipped).astype(jnp.bfloat16)
    gate_grad = (slope * cot_hidden.astype(jnp.float32)).astype(jnp.bfloat16)
    kernel_flip = jnp.transpose(conv_weight[::-1, ::-1], (0, 1, 3, 2))
    features_grad = (cot_hidden.astype(jnp.float32) + spatial_conv(gate_grad, kernel_flip)).astype(
        jnp.bfloat16
    )
    return (updated, features_grad)


def solution(mesh):
    return jax.shard_map(
        on_device,
        mesh=mesh,
        in_specs=(
            P(None, None, "row", ("ta", "col")),
            P(),
            P(),
            P(),
            P(),
            P(("ta", "col"), "row", None),
            P(("ta", "col"), "row", None),
            P(),
            P(("ta", "col"), None, "row", None),
        ),
        out_specs=(P(("ta", "col"), None, "row", None), P(None, None, "row", ("ta", "col"))),
        check_vma=False,
    )
```

```python
import jax
import jax.numpy as jnp
from jax import lax
from jax.sharding import PartitionSpec as P


def with_halo(array, sides, width):
    for axis, dim in sides:
        devices, length = (lax.axis_size(axis), array.shape[dim])
        up = [(i, (i + 1) % devices) for i in range(devices - 1)]
        down = [(j, i) for i, j in up]
        last = lax.slice_in_dim(array, length - width, length, axis=dim)
        initial = lax.slice_in_dim(array, 0, width, axis=dim)
        before = lax.ppermute(last, axis, up)
        after = lax.ppermute(initial, axis, down)
        array = jnp.concatenate([before, array, after], axis=dim)
    return array


def row_halo(field_in):
    return with_halo(field_in, (("row", 2),), 1)


def halo_conv(rows, kernel):
    padded = with_halo(rows, ((("ta", "col"), 3),), 1)
    return lax.conv_general_dilated(
        padded,
        kernel,
        window_strides=(1, 1),
        padding="VALID",
        dimension_numbers=("NCHW", "HWIO", "NCHW"),
        preferred_element_type=jnp.float32,
    )


def spatial_conv(field_in, kernel):
    return halo_conv(row_halo(field_in), kernel)


def to_time(field_in):
    return lax.all_to_all(field_in, ("ta", "col"), split_axis=0, concat_axis=3, tiled=True)


def to_space(field_in):
    return lax.all_to_all(field_in, ("ta", "col"), split_axis=3, concat_axis=0, tiled=True)


def time_mix(frames_in, time_taps):
    frame_count = frames_in.shape[0]
    padded = jnp.pad(frames_in, ((2, 2), (0, 0), (0, 0), (0, 0)))
    summed = jnp.zeros(frames_in.shape, jnp.float32)
    for tap_index in range(5):
        summed = summed + time_taps[None, :, tap_index, None, None] * padded[
            tap_index : tap_index + frame_count
        ].astype(jnp.float32)
    return summed


def gelu_exact(values_in):
    return jax.nn.gelu(values_in, approximate=False)


def shift_bits(dispersion, largest):
    bits = largest.bit_length()
    return [((dispersion >> k) & 1).astype(bool)[None, :, None, None] for k in range(bits)]


def disperse(masked, bits, width_wide):
    moved = jnp.pad(masked, ((0, 0),) * 3 + ((0, width_wide - masked.shape[-1]),))
    for k, bit in enumerate(bits):
        step = 1 << k
        later = jnp.pad(moved[..., :-step], ((0, 0),) * 3 + ((step, 0),))
        moved = jnp.where(bit, later, moved)
    return jnp.sum(moved, axis=1)


def undisperse(field_in, bits, width_keep):
    moved = jnp.broadcast_to(
        field_in[:, None], (field_in.shape[0], bits[0].shape[1]) + field_in.shape[1:]
    )
    for k, bit in enumerate(bits):
        step = 1 << k
        earlier = jnp.pad(moved[..., step:], ((0, 0),) * 3 + ((0, step),))
        moved = jnp.where(bit, earlier, moved)
    return moved[..., :width_keep]


def on_device(
    features,
    conv_weight,
    time_weight,
    band_out,
    band_input_weight,
    measured,
    aperture,
    dispersion,
    update_cot,
):
    width_keep = aperture.shape[-1]
    width_wide = measured.shape[-1]
    bits = shift_bits(dispersion, width_wide - width_keep)
    mask_float = aperture.astype(jnp.float32)[:, None]
    band_cot = jnp.einsum(
        "fcqw,bc->fbqw", update_cot, band_input_weight, preferred_element_type=jnp.float32
    )
    resid_grad = disperse(band_cot * mask_float, bits, width_wide)
    band_grad = (-(undisperse(resid_grad, bits, width_keep) * mask_float)).astype(jnp.bfloat16)
    cot_temporal = (
        update_cot.astype(jnp.float32)
        + jnp.einsum("fbqw,cb->fcqw", band_grad, band_out, preferred_element_type=jnp.float32)
    ).astype(jnp.bfloat16)
    feature_rows = row_halo(features)
    feature_rows, cot_temporal = lax.optimization_barrier((feature_rows, cot_temporal))
    pre_act = halo_conv(feature_rows, conv_weight)
    gelu_value, pullback = jax.vjp(gelu_exact, pre_act)
    slope = pullback(jnp.ones_like(pre_act))[0]
    hidden_state = (features.astype(jnp.float32) + gelu_value).astype(jnp.bfloat16)
    temporal = to_time(time_mix(hidden_state, time_weight).astype(jnp.bfloat16))
    band_vals = jnp.einsum("fcqw,cb->fbqw", temporal, band_out, preferred_element_type=jnp.float32)
    masked_band_sum = disperse(band_vals * mask_float, bits, width_wide)
    residual_error = measured - masked_band_sum
    back_proj = (undisperse(residual_error, bits, width_keep) * mask_float).astype(jnp.bfloat16)
    updated = (
        temporal.astype(jnp.float32)
        + jnp.einsum(
            "fbqw,bc->fcqw", back_proj, band_input_weight, preferred_element_type=jnp.float32
        )
    ).astype(jnp.bfloat16)
    flipped = time_weight[:, ::-1]
    cot_space, slope = lax.optimization_barrier((to_space(cot_temporal), slope))
    cot_hidden = time_mix(cot_space, flipped).astype(jnp.bfloat16)
    gate_grad = (slope * cot_hidden.astype(jnp.float32)).astype(jnp.bfloat16)
    kernel_flip = jnp.transpose(conv_weight[::-1, ::-1], (0, 1, 3, 2))
    features_grad = (cot_hidden.astype(jnp.float32) + spatial_conv(gate_grad, kernel_flip)).astype(
        jnp.bfloat16
    )
    return (updated, features_grad)


def solution(mesh):
    return jax.shard_map(
        on_device,
        mesh=mesh,
        in_specs=(
            P(None, None, "row", ("ta", "col")),
            P(),
            P(),
            P(),
            P(),
            P(("ta", "col"), "row", None),
            P(("ta", "col"), "row", None),
            P(),
            P(("ta", "col"), None, "row", None),
        ),
        out_specs=(P(("ta", "col"), None, "row", None), P(None, None, "row", ("ta", "col"))),
        check_vma=False,
    )
```

```python
import jax
import jax.numpy as jnp
from jax import lax
from jax.sharding import PartitionSpec as P


def with_halo(array, sides, width):
    for axis, dim in sides:
        devices, length = (lax.axis_size(axis), array.shape[dim])
        up = [(i, (i + 1) % devices) for i in range(devices - 1)]
        down = [(j, i) for i, j in up]
        last = lax.slice_in_dim(array, length - width, length, axis=dim)
        initial = lax.slice_in_dim(array, 0, width, axis=dim)
        before = lax.ppermute(last, axis, up)
        after = lax.ppermute(initial, axis, down)
        array = jnp.concatenate([before, array, after], axis=dim)
    return array


def row_halo(field_in):
    return with_halo(field_in, (("row", 2),), 1)


def halo_conv(rows, kernel):
    padded = with_halo(rows, ((("ta", "col"), 3),), 1)
    return lax.conv_general_dilated(
        padded,
        kernel,
        window_strides=(1, 1),
        padding="VALID",
        dimension_numbers=("NCHW", "HWIO", "NCHW"),
        preferred_element_type=jnp.float32,
    )


def spatial_conv(field_in, kernel):
    return halo_conv(row_halo(field_in), kernel)


def to_time(field_in):
    return lax.all_to_all(field_in, ("ta", "col"), split_axis=0, concat_axis=3, tiled=True)


def to_space(field_in):
    return lax.all_to_all(field_in, ("ta", "col"), split_axis=3, concat_axis=0, tiled=True)


def time_mix(frames_in, time_taps):
    frame_count = frames_in.shape[0]
    padded = jnp.pad(frames_in, ((2, 2), (0, 0), (0, 0), (0, 0)))
    summed = jnp.zeros(frames_in.shape, jnp.float32)
    for tap_index in range(5):
        summed = summed + time_taps[None, :, tap_index, None, None] * padded[
            tap_index : tap_index + frame_count
        ].astype(jnp.float32)
    return summed


def gelu_exact(values_in):
    return jax.nn.gelu(values_in, approximate=False)


def shift_bits(dispersion, largest):
    bits = largest.bit_length()
    return [((dispersion >> k) & 1).astype(bool)[None, :, None, None] for k in range(bits)]


def disperse(masked, bits, width_wide):
    moved = jnp.pad(masked, ((0, 0),) * 3 + ((0, width_wide - masked.shape[-1]),))
    for k, bit in enumerate(bits):
        step = 1 << k
        later = jnp.pad(moved[..., :-step], ((0, 0),) * 3 + ((step, 0),))
        moved = jnp.where(bit, later, moved)
    return jnp.sum(moved, axis=1)


def undisperse(field_in, bits, width_keep):
    moved = jnp.broadcast_to(
        field_in[:, None], (field_in.shape[0], bits[0].shape[1]) + field_in.shape[1:]
    )
    for k, bit in enumerate(bits):
        step = 1 << k
        earlier = jnp.pad(moved[..., step:], ((0, 0),) * 3 + ((0, step),))
        moved = jnp.where(bit, earlier, moved)
    return moved[..., :width_keep]


def on_device(
    features,
    conv_weight,
    time_weight,
    band_out,
    band_input_weight,
    measured,
    aperture,
    dispersion,
    update_cot,
):
    width_keep = aperture.shape[-1]
    width_wide = measured.shape[-1]
    bits = shift_bits(dispersion, width_wide - width_keep)
    mask_float = aperture.astype(jnp.float32)[:, None]
    band_cot = jnp.einsum(
        "fcqw,bc->fbqw", update_cot, band_input_weight, preferred_element_type=jnp.float32
    )
    resid_grad = disperse(band_cot * mask_float, bits, width_wide)
    band_grad = (-(undisperse(resid_grad, bits, width_keep) * mask_float)).astype(jnp.bfloat16)
    cot_temporal = (
        update_cot.astype(jnp.float32)
        + jnp.einsum("fbqw,cb->fcqw", band_grad, band_out, preferred_element_type=jnp.float32)
    ).astype(jnp.bfloat16)
    feature_rows = row_halo(features)
    feature_rows, cot_temporal = lax.optimization_barrier((feature_rows, cot_temporal))
    pre_act = halo_conv(feature_rows, conv_weight)
    gelu_value, pullback = jax.vjp(gelu_exact, pre_act)
    slope = pullback(jnp.ones_like(pre_act))[0]
    hidden_state = (features.astype(jnp.float32) + gelu_value).astype(jnp.bfloat16)
    temporal_space = time_mix(hidden_state, time_weight).astype(jnp.bfloat16)
    flipped = time_weight[:, ::-1]
    cot_space, slope, temporal_space = lax.optimization_barrier(
        (to_space(cot_temporal), slope, temporal_space)
    )
    temporal = to_time(temporal_space)
    band_vals = jnp.einsum("fcqw,cb->fbqw", temporal, band_out, preferred_element_type=jnp.float32)
    masked_band_sum = disperse(band_vals * mask_float, bits, width_wide)
    residual_error = measured - masked_band_sum
    back_proj = (undisperse(residual_error, bits, width_keep) * mask_float).astype(jnp.bfloat16)
    updated = (
        temporal.astype(jnp.float32)
        + jnp.einsum(
            "fbqw,bc->fcqw", back_proj, band_input_weight, preferred_element_type=jnp.float32
        )
    ).astype(jnp.bfloat16)
    cot_hidden = time_mix(cot_space, flipped).astype(jnp.bfloat16)
    gate_grad = (slope * cot_hidden.astype(jnp.float32)).astype(jnp.bfloat16)
    kernel_flip = jnp.transpose(conv_weight[::-1, ::-1], (0, 1, 3, 2))
    features_grad = (cot_hidden.astype(jnp.float32) + spatial_conv(gate_grad, kernel_flip)).astype(
        jnp.bfloat16
    )
    return (updated, features_grad)


def solution(mesh):
    return jax.shard_map(
        on_device,
        mesh=mesh,
        in_specs=(
            P(None, None, "row", ("ta", "col")),
            P(),
            P(),
            P(),
            P(),
            P(("ta", "col"), "row", None),
            P(("ta", "col"), "row", None),
            P(),
            P(("ta", "col"), None, "row", None),
        ),
        out_specs=(P(("ta", "col"), None, "row", None), P(None, None, "row", ("ta", "col"))),
        check_vma=False,
    )
```

```python
import jax
import jax.numpy as jnp
from jax import lax
from jax.sharding import PartitionSpec as P


def with_halo(array, sides, width):
    for axis, dim in sides:
        devices, length = (lax.axis_size(axis), array.shape[dim])
        up = [(i, (i + 1) % devices) for i in range(devices - 1)]
        down = [(j, i) for i, j in up]
        last = lax.slice_in_dim(array, length - width, length, axis=dim)
        initial = lax.slice_in_dim(array, 0, width, axis=dim)
        before = lax.ppermute(last, axis, up)
        after = lax.ppermute(initial, axis, down)
        array = jnp.concatenate([before, array, after], axis=dim)
    return array


def row_halo(field_in):
    return with_halo(field_in, (("row", 2),), 1)


def valid_conv(padded, kernel):
    return lax.conv_general_dilated(
        padded,
        kernel,
        window_strides=(1, 1),
        padding="VALID",
        dimension_numbers=("NCHW", "HWIO", "NCHW"),
        preferred_element_type=jnp.float32,
    )


def halo_conv(rows, kernel):
    return valid_conv(with_halo(rows, ((("ta", "col"), 3),), 1), kernel)


def to_time(field_in):
    return lax.all_to_all(field_in, ("ta", "col"), split_axis=0, concat_axis=3, tiled=True)


def to_space(field_in):
    return lax.all_to_all(field_in, ("ta", "col"), split_axis=3, concat_axis=0, tiled=True)


def time_mix(frames_in, time_taps):
    frame_count = frames_in.shape[0]
    padded = jnp.pad(frames_in, ((2, 2), (0, 0), (0, 0), (0, 0)))
    summed = jnp.zeros(frames_in.shape, jnp.float32)
    for tap_index in range(5):
        summed = summed + time_taps[None, :, tap_index, None, None] * padded[
            tap_index : tap_index + frame_count
        ].astype(jnp.float32)
    return summed


def gelu_exact(values_in):
    return jax.nn.gelu(values_in, approximate=False)


def shift_bits(dispersion, largest):
    bits = largest.bit_length()
    return [((dispersion >> k) & 1).astype(bool)[None, :, None, None] for k in range(bits)]


def disperse(masked, bits, width_wide):
    moved = jnp.pad(masked, ((0, 0),) * 3 + ((0, width_wide - masked.shape[-1]),))
    for k, bit in enumerate(bits):
        step = 1 << k
        later = jnp.pad(moved[..., :-step], ((0, 0),) * 3 + ((step, 0),))
        moved = jnp.where(bit, later, moved)
    return jnp.sum(moved, axis=1)


def undisperse(field_in, bits, width_keep):
    moved = jnp.broadcast_to(
        field_in[:, None], (field_in.shape[0], bits[0].shape[1]) + field_in.shape[1:]
    )
    for k, bit in enumerate(bits):
        step = 1 << k
        earlier = jnp.pad(moved[..., step:], ((0, 0),) * 3 + ((0, step),))
        moved = jnp.where(bit, earlier, moved)
    return moved[..., :width_keep]


def on_device(
    features,
    conv_weight,
    time_weight,
    band_out,
    band_input_weight,
    measured,
    aperture,
    dispersion,
    update_cot,
):
    width_keep = aperture.shape[-1]
    width_wide = measured.shape[-1]
    bits = shift_bits(dispersion, width_wide - width_keep)
    mask_float = aperture.astype(jnp.float32)[:, None]
    band_cot = jnp.einsum(
        "fcqw,bc->fbqw", update_cot, band_input_weight, preferred_element_type=jnp.float32
    )
    resid_grad = disperse(band_cot * mask_float, bits, width_wide)
    band_grad = (-(undisperse(resid_grad, bits, width_keep) * mask_float)).astype(jnp.bfloat16)
    cot_temporal = (
        update_cot.astype(jnp.float32)
        + jnp.einsum("fbqw,cb->fcqw", band_grad, band_out, preferred_element_type=jnp.float32)
    ).astype(jnp.bfloat16)
    feature_rows = row_halo(features)
    feature_rows, cot_temporal = lax.optimization_barrier((feature_rows, cot_temporal))
    pre_act = halo_conv(feature_rows, conv_weight)
    gelu_value, pullback = jax.vjp(gelu_exact, pre_act)
    slope = pullback(jnp.ones_like(pre_act))[0]
    hidden_state = (features.astype(jnp.float32) + gelu_value).astype(jnp.bfloat16)
    temporal_space = time_mix(hidden_state, time_weight).astype(jnp.bfloat16)
    flipped = time_weight[:, ::-1]
    cot_space, slope, temporal_space = lax.optimization_barrier(
        (to_space(cot_temporal), slope, temporal_space)
    )
    temporal = to_time(temporal_space)
    band_vals = jnp.einsum("fcqw,cb->fbqw", temporal, band_out, preferred_element_type=jnp.float32)
    masked_band_sum = disperse(band_vals * mask_float, bits, width_wide)
    residual_error = measured - masked_band_sum
    back_proj = (undisperse(residual_error, bits, width_keep) * mask_float).astype(jnp.bfloat16)
    updated = (
        temporal.astype(jnp.float32)
        + jnp.einsum(
            "fbqw,bc->fcqw", back_proj, band_input_weight, preferred_element_type=jnp.float32
        )
    ).astype(jnp.bfloat16)
    cot_hidden = time_mix(cot_space, flipped).astype(jnp.bfloat16)
    gate_grad = (slope * cot_hidden.astype(jnp.float32)).astype(jnp.bfloat16)
    kernel_flip = jnp.transpose(conv_weight[::-1, ::-1], (0, 1, 3, 2))
    gate_cols = with_halo(gate_grad, ((("ta", "col"), 3),), 1)
    features_grad = (
        cot_hidden.astype(jnp.float32) + valid_conv(row_halo(gate_cols), kernel_flip)
    ).astype(jnp.bfloat16)
    return (updated, features_grad)


def solution(mesh):
    return jax.shard_map(
        on_device,
        mesh=mesh,
        in_specs=(
            P(None, None, "row", ("ta", "col")),
            P(),
            P(),
            P(),
            P(),
            P(("ta", "col"), "row", None),
            P(("ta", "col"), "row", None),
            P(),
            P(("ta", "col"), None, "row", None),
        ),
        out_specs=(P(("ta", "col"), None, "row", None), P(None, None, "row", ("ta", "col"))),
        check_vma=False,
    )
```

```python
import jax
import jax.numpy as jnp
from jax import lax
from jax.sharding import PartitionSpec as P


def with_halo(array, sides, width):
    for axis, dim in sides:
        devices, length = (lax.axis_size(axis), array.shape[dim])
        up = [(i, (i + 1) % devices) for i in range(devices - 1)]
        down = [(j, i) for i, j in up]
        last = lax.slice_in_dim(array, length - width, length, axis=dim)
        initial = lax.slice_in_dim(array, 0, width, axis=dim)
        before = lax.ppermute(last, axis, up)
        after = lax.ppermute(initial, axis, down)
        array = jnp.concatenate([before, array, after], axis=dim)
    return array


def row_halo(field_in):
    return with_halo(field_in, (("row", 2),), 1)


def halo_conv(rows, kernel):
    padded = with_halo(rows, ((("ta", "col"), 3),), 1)
    return lax.conv_general_dilated(
        padded,
        kernel,
        window_strides=(1, 1),
        padding="VALID",
        dimension_numbers=("NCHW", "HWIO", "NCHW"),
        preferred_element_type=jnp.float32,
    )


def spatial_conv(field_in, kernel):
    return halo_conv(row_halo(field_in), kernel)


def lane_rows(block):
    lanes = 128
    return block.reshape(block.shape[0], -1, lanes)


def to_time(field_in):
    blocks = lax.axis_size(("ta", "col"))
    frames = field_in.shape[0] // blocks
    sent = lane_rows(field_in.reshape((blocks, frames * field_in.shape[1]) + field_in.shape[2:]))
    got = lax.all_to_all(sent, ("ta", "col"), split_axis=0, concat_axis=0, tiled=True)
    got = got.reshape((blocks, frames) + field_in.shape[1:])
    return jnp.moveaxis(got, 0, 3).reshape(
        (frames,) + field_in.shape[1:3] + (blocks * field_in.shape[3],)
    )


def to_space(field_in):
    blocks = lax.axis_size(("ta", "col"))
    width = field_in.shape[3] // blocks
    split = field_in.reshape(field_in.shape[:3] + (blocks, width))
    sent = lane_rows(jnp.moveaxis(split, 3, 0))
    got = lax.all_to_all(sent, ("ta", "col"), split_axis=0, concat_axis=0, tiled=True)
    return got.reshape((blocks * field_in.shape[0],) + field_in.shape[1:3] + (width,))


def time_mix(frames_in, time_taps):
    frame_count = frames_in.shape[0]
    padded = jnp.pad(frames_in, ((2, 2), (0, 0), (0, 0), (0, 0)))
    summed = jnp.zeros(frames_in.shape, jnp.float32)
    for tap_index in range(5):
        summed = summed + time_taps[None, :, tap_index, None, None] * padded[
            tap_index : tap_index + frame_count
        ].astype(jnp.float32)
    return summed


def gelu_exact(values_in):
    return jax.nn.gelu(values_in, approximate=False)


def shift_bits(dispersion, largest):
    bits = largest.bit_length()
    return [((dispersion >> k) & 1).astype(bool)[None, :, None, None] for k in range(bits)]


def disperse(masked, bits, width_wide):
    moved = jnp.pad(masked, ((0, 0),) * 3 + ((0, width_wide - masked.shape[-1]),))
    for k, bit in enumerate(bits):
        step = 1 << k
        later = jnp.pad(moved[..., :-step], ((0, 0),) * 3 + ((step, 0),))
        moved = jnp.where(bit, later, moved)
    return jnp.sum(moved, axis=1)


def undisperse(field_in, bits, width_keep):
    moved = jnp.broadcast_to(
        field_in[:, None], (field_in.shape[0], bits[0].shape[1]) + field_in.shape[1:]
    )
    for k, bit in enumerate(bits):
        step = 1 << k
        earlier = jnp.pad(moved[..., step:], ((0, 0),) * 3 + ((0, step),))
        moved = jnp.where(bit, earlier, moved)
    return moved[..., :width_keep]


def on_device(
    features,
    conv_weight,
    time_weight,
    band_out,
    band_input_weight,
    measured,
    aperture,
    dispersion,
    update_cot,
):
    width_keep = aperture.shape[-1]
    width_wide = measured.shape[-1]
    bits = shift_bits(dispersion, width_wide - width_keep)
    mask_float = aperture.astype(jnp.float32)[:, None]
    band_cot = jnp.einsum(
        "fcqw,bc->fbqw", update_cot, band_input_weight, preferred_element_type=jnp.float32
    )
    resid_grad = disperse(band_cot * mask_float, bits, width_wide)
    band_grad = (-(undisperse(resid_grad, bits, width_keep) * mask_float)).astype(jnp.bfloat16)
    cot_temporal = (
        update_cot.astype(jnp.float32)
        + jnp.einsum("fbqw,cb->fcqw", band_grad, band_out, preferred_element_type=jnp.float32)
    ).astype(jnp.bfloat16)
    feature_rows = row_halo(features)
    feature_rows, cot_temporal = lax.optimization_barrier((feature_rows, cot_temporal))
    pre_act = halo_conv(feature_rows, conv_weight)
    gelu_value, pullback = jax.vjp(gelu_exact, pre_act)
    slope = pullback(jnp.ones_like(pre_act))[0]
    hidden_state = (features.astype(jnp.float32) + gelu_value).astype(jnp.bfloat16)
    temporal_space = time_mix(hidden_state, time_weight).astype(jnp.bfloat16)
    flipped = time_weight[:, ::-1]
    cot_space, slope, temporal_space = lax.optimization_barrier(
        (to_space(cot_temporal), slope, temporal_space)
    )
    temporal = to_time(temporal_space)
    band_vals = jnp.einsum("fcqw,cb->fbqw", temporal, band_out, preferred_element_type=jnp.float32)
    masked_band_sum = disperse(band_vals * mask_float, bits, width_wide)
    residual_error = measured - masked_band_sum
    back_proj = (undisperse(residual_error, bits, width_keep) * mask_float).astype(jnp.bfloat16)
    updated = (
        temporal.astype(jnp.float32)
        + jnp.einsum(
            "fbqw,bc->fcqw", back_proj, band_input_weight, preferred_element_type=jnp.float32
        )
    ).astype(jnp.bfloat16)
    cot_hidden = time_mix(cot_space, flipped).astype(jnp.bfloat16)
    gate_grad = (slope * cot_hidden.astype(jnp.float32)).astype(jnp.bfloat16)
    kernel_flip = jnp.transpose(conv_weight[::-1, ::-1], (0, 1, 3, 2))
    features_grad = (cot_hidden.astype(jnp.float32) + spatial_conv(gate_grad, kernel_flip)).astype(
        jnp.bfloat16
    )
    return (updated, features_grad)


def solution(mesh):
    return jax.shard_map(
        on_device,
        mesh=mesh,
        in_specs=(
            P(None, None, "row", ("ta", "col")),
            P(),
            P(),
            P(),
            P(),
            P(("ta", "col"), "row", None),
            P(("ta", "col"), "row", None),
            P(),
            P(("ta", "col"), None, "row", None),
        ),
        out_specs=(P(("ta", "col"), None, "row", None), P(None, None, "row", ("ta", "col"))),
        check_vma=False,
    )
```

```python
import jax
import jax.numpy as jnp
from jax import lax
from jax.sharding import PartitionSpec as P


def with_halo(array, sides, width, dense=False):
    for axis, dim in sides:
        devices, length = (lax.axis_size(axis), array.shape[dim])
        up = [(i, (i + 1) % devices) for i in range(devices - 1)]
        down = [(j, i) for i, j in up]
        last = lax.slice_in_dim(array, length - width, length, axis=dim)
        initial = lax.slice_in_dim(array, 0, width, axis=dim)
        if dense:
            before = lax.ppermute(lane_rows(last[None]), axis, up).reshape(last.shape)
            after = lax.ppermute(lane_rows(initial[None]), axis, down).reshape(initial.shape)
        else:
            before = lax.ppermute(last, axis, up)
            after = lax.ppermute(initial, axis, down)
        array = jnp.concatenate([before, array, after], axis=dim)
    return array


def row_halo(field_in):
    return with_halo(field_in, (("row", 2),), 1)


def halo_conv(rows, kernel):
    padded = with_halo(rows, ((("ta", "col"), 3),), 1)
    return lax.conv_general_dilated(
        padded,
        kernel,
        window_strides=(1, 1),
        padding="VALID",
        dimension_numbers=("NCHW", "HWIO", "NCHW"),
        preferred_element_type=jnp.float32,
    )


def lane_rows(block):
    lanes = 128
    return block.reshape(block.shape[0], -1, lanes)


def to_time(field_in):
    blocks = lax.axis_size(("ta", "col"))
    frames = field_in.shape[0] // blocks
    sent = lane_rows(field_in.reshape((blocks, frames * field_in.shape[1]) + field_in.shape[2:]))
    got = lax.all_to_all(sent, ("ta", "col"), split_axis=0, concat_axis=0, tiled=True)
    got = got.reshape((blocks, frames) + field_in.shape[1:])
    return jnp.moveaxis(got, 0, 3).reshape(
        (frames,) + field_in.shape[1:3] + (blocks * field_in.shape[3],)
    )


def to_space(field_in):
    blocks = lax.axis_size(("ta", "col"))
    width = field_in.shape[3] // blocks
    split = field_in.reshape(field_in.shape[:3] + (blocks, width))
    sent = lane_rows(jnp.moveaxis(split, 3, 0))
    got = lax.all_to_all(sent, ("ta", "col"), split_axis=0, concat_axis=0, tiled=True)
    return got.reshape((blocks * field_in.shape[0],) + field_in.shape[1:3] + (width,))


def time_mix(frames_in, time_taps):
    frame_count = frames_in.shape[0]
    padded = jnp.pad(frames_in, ((2, 2), (0, 0), (0, 0), (0, 0)))
    summed = jnp.zeros(frames_in.shape, jnp.float32)
    for tap_index in range(5):
        summed = summed + time_taps[None, :, tap_index, None, None] * padded[
            tap_index : tap_index + frame_count
        ].astype(jnp.float32)
    return summed


def gelu_exact(values_in):
    return jax.nn.gelu(values_in, approximate=False)


def shift_bits(dispersion, largest):
    bits = largest.bit_length()
    return [((dispersion >> k) & 1).astype(bool)[None, :, None, None] for k in range(bits)]


def disperse(masked, bits, width_wide):
    moved = jnp.pad(masked, ((0, 0),) * 3 + ((0, width_wide - masked.shape[-1]),))
    for k, bit in enumerate(bits):
        step = 1 << k
        later = jnp.pad(moved[..., :-step], ((0, 0),) * 3 + ((step, 0),))
        moved = jnp.where(bit, later, moved)
    return jnp.sum(moved, axis=1)


def undisperse(field_in, bits, width_keep):
    moved = jnp.broadcast_to(
        field_in[:, None], (field_in.shape[0], bits[0].shape[1]) + field_in.shape[1:]
    )
    for k, bit in enumerate(bits):
        step = 1 << k
        earlier = jnp.pad(moved[..., step:], ((0, 0),) * 3 + ((0, step),))
        moved = jnp.where(bit, earlier, moved)
    return moved[..., :width_keep]


def on_device(
    features,
    conv_weight,
    time_weight,
    band_out,
    band_input_weight,
    measured,
    aperture,
    dispersion,
    update_cot,
):
    width_keep = aperture.shape[-1]
    width_wide = measured.shape[-1]
    bits = shift_bits(dispersion, width_wide - width_keep)
    mask_float = aperture.astype(jnp.float32)[:, None]
    band_cot = jnp.einsum(
        "fcqw,bc->fbqw", update_cot, band_input_weight, preferred_element_type=jnp.float32
    )
    resid_grad = disperse(band_cot * mask_float, bits, width_wide)
    band_grad = (-(undisperse(resid_grad, bits, width_keep) * mask_float)).astype(jnp.bfloat16)
    cot_temporal = (
        update_cot.astype(jnp.float32)
        + jnp.einsum("fbqw,cb->fcqw", band_grad, band_out, preferred_element_type=jnp.float32)
    ).astype(jnp.bfloat16)
    feature_rows = row_halo(features)
    feature_rows, cot_temporal = lax.optimization_barrier((feature_rows, cot_temporal))
    pre_act = halo_conv(feature_rows, conv_weight)
    gelu_value, pullback = jax.vjp(gelu_exact, pre_act)
    slope = pullback(jnp.ones_like(pre_act))[0]
    hidden_state = (features.astype(jnp.float32) + gelu_value).astype(jnp.bfloat16)
    temporal_space = time_mix(hidden_state, time_weight).astype(jnp.bfloat16)
    flipped = time_weight[:, ::-1]
    cot_space, slope, temporal_space = lax.optimization_barrier(
        (to_space(cot_temporal), slope, temporal_space)
    )
    temporal = to_time(temporal_space)
    band_vals = jnp.einsum("fcqw,cb->fbqw", temporal, band_out, preferred_element_type=jnp.float32)
    masked_band_sum = disperse(band_vals * mask_float, bits, width_wide)
    residual_error = measured - masked_band_sum
    back_proj = (undisperse(residual_error, bits, width_keep) * mask_float).astype(jnp.bfloat16)
    updated = (
        temporal.astype(jnp.float32)
        + jnp.einsum(
            "fbqw,bc->fcqw", back_proj, band_input_weight, preferred_element_type=jnp.float32
        )
    ).astype(jnp.bfloat16)
    cot_hidden = time_mix(cot_space, flipped).astype(jnp.bfloat16)
    gate_grad = (slope * cot_hidden.astype(jnp.float32)).astype(jnp.bfloat16)
    kernel_flip = jnp.transpose(conv_weight[::-1, ::-1], (0, 1, 3, 2))
    gate_rows = with_halo(gate_grad, (("row", 2),), 1, dense=True)
    features_grad = (cot_hidden.astype(jnp.float32) + halo_conv(gate_rows, kernel_flip)).astype(
        jnp.bfloat16
    )
    return (updated, features_grad)


def solution(mesh):
    return jax.shard_map(
        on_device,
        mesh=mesh,
        in_specs=(
            P(None, None, "row", ("ta", "col")),
            P(),
            P(),
            P(),
            P(),
            P(("ta", "col"), "row", None),
            P(("ta", "col"), "row", None),
            P(),
            P(("ta", "col"), None, "row", None),
        ),
        out_specs=(P(("ta", "col"), None, "row", None), P(None, None, "row", ("ta", "col"))),
        check_vma=False,
    )
```

```python
import jax
import jax.numpy as jnp
from jax import lax
from jax.sharding import PartitionSpec as P


def with_halo(array, sides, width):
    for axis, dim in sides:
        devices, length = (lax.axis_size(axis), array.shape[dim])
        up = [(i, (i + 1) % devices) for i in range(devices - 1)]
        down = [(j, i) for i, j in up]
        last = lax.slice_in_dim(array, length - width, length, axis=dim)
        initial = lax.slice_in_dim(array, 0, width, axis=dim)
        before = lax.ppermute(last, axis, up)
        after = lax.ppermute(initial, axis, down)
        array = jnp.concatenate([before, array, after], axis=dim)
    return array


def row_halo(field_in):
    return with_halo(field_in, (("row", 2),), 1)


def halo_conv(rows, kernel):
    padded = with_halo(rows, ((("ta", "col"), 3),), 1)
    return lax.conv_general_dilated(
        padded,
        kernel,
        window_strides=(1, 1),
        padding="VALID",
        dimension_numbers=("NCHW", "HWIO", "NCHW"),
        preferred_element_type=jnp.float32,
    )


def spatial_conv(field_in, kernel):
    return halo_conv(row_halo(field_in), kernel)


def lane_rows(block):
    lanes = 128
    return block.reshape(block.shape[0], -1, lanes)


def to_time(field_in):
    blocks = lax.axis_size(("ta", "col"))
    frames = field_in.shape[0] // blocks
    sent = lane_rows(field_in.reshape((blocks, frames * field_in.shape[1]) + field_in.shape[2:]))
    got = lax.all_to_all(sent, ("ta", "col"), split_axis=0, concat_axis=0, tiled=True)
    got = got.reshape((blocks, frames) + field_in.shape[1:])
    return jnp.moveaxis(got, 0, 3).reshape(
        (frames,) + field_in.shape[1:3] + (blocks * field_in.shape[3],)
    )


def to_space(field_in):
    blocks = lax.axis_size(("ta", "col"))
    width = field_in.shape[3] // blocks
    split = field_in.reshape(field_in.shape[:3] + (blocks, width))
    sent = lane_rows(jnp.moveaxis(split, 3, 0))
    got = lax.all_to_all(sent, ("ta", "col"), split_axis=0, concat_axis=0, tiled=True)
    return got.reshape((blocks * field_in.shape[0],) + field_in.shape[1:3] + (width,))


def time_mix(frames_in, time_taps):
    frame_count = frames_in.shape[0]
    padded = jnp.pad(frames_in, ((2, 2), (0, 0), (0, 0), (0, 0)))
    summed = jnp.zeros(frames_in.shape, jnp.float32)
    for tap_index in range(5):
        summed = summed + time_taps[None, :, tap_index, None, None] * padded[
            tap_index : tap_index + frame_count
        ].astype(jnp.float32)
    return summed


def gelu_exact(values_in):
    return jax.nn.gelu(values_in, approximate=False)


def shift_bits(dispersion, largest):
    bits = largest.bit_length()
    return [((dispersion >> k) & 1).astype(bool)[None, :, None, None] for k in range(bits)]


def disperse(masked, bits, width_wide):
    moved = jnp.pad(masked, ((0, 0),) * 3 + ((0, width_wide - masked.shape[-1]),))
    for k, bit in enumerate(bits):
        step = 1 << k
        later = jnp.pad(moved[..., :-step], ((0, 0),) * 3 + ((step, 0),))
        moved = jnp.where(bit, later, moved)
    return jnp.sum(moved, axis=1)


def undisperse(field_in, bits, width_keep):
    moved = jnp.broadcast_to(
        field_in[:, None], (field_in.shape[0], bits[0].shape[1]) + field_in.shape[1:]
    )
    for k, bit in enumerate(bits):
        step = 1 << k
        earlier = jnp.pad(moved[..., step:], ((0, 0),) * 3 + ((0, step),))
        moved = jnp.where(bit, earlier, moved)
    return moved[..., :width_keep]


def on_device(
    features,
    conv_weight,
    time_weight,
    band_out,
    band_input_weight,
    measured,
    aperture,
    dispersion,
    update_cot,
):
    width_keep = aperture.shape[-1]
    width_wide = measured.shape[-1]
    bits = shift_bits(dispersion, width_wide - width_keep)
    mask_float = aperture.astype(jnp.float32)[:, None]
    band_cot = jnp.einsum(
        "fcqw,bc->fbqw", update_cot, band_input_weight, preferred_element_type=jnp.float32
    )
    resid_grad = disperse(band_cot * mask_float, bits, width_wide)
    band_grad = (-(undisperse(resid_grad, bits, width_keep) * mask_float)).astype(jnp.bfloat16)
    cot_temporal = (
        update_cot.astype(jnp.float32)
        + jnp.einsum("fbqw,cb->fcqw", band_grad, band_out, preferred_element_type=jnp.float32)
    ).astype(jnp.bfloat16)
    feature_rows = row_halo(features)
    feature_rows, cot_temporal = lax.optimization_barrier((feature_rows, cot_temporal))
    pre_act = halo_conv(feature_rows, conv_weight)
    gelu_value, pullback = jax.vjp(gelu_exact, pre_act)
    slope = pullback(jnp.ones_like(pre_act))[0]
    hidden_state = (features.astype(jnp.float32) + gelu_value).astype(jnp.bfloat16)
    temporal_space = time_mix(hidden_state, time_weight).astype(jnp.bfloat16)
    flipped = time_weight[:, ::-1]
    cot_space, slope = lax.optimization_barrier((to_space(cot_temporal), slope))
    temporal = to_time(temporal_space)
    band_vals = jnp.einsum("fcqw,cb->fbqw", temporal, band_out, preferred_element_type=jnp.float32)
    masked_band_sum = disperse(band_vals * mask_float, bits, width_wide)
    residual_error = measured - masked_band_sum
    back_proj = (undisperse(residual_error, bits, width_keep) * mask_float).astype(jnp.bfloat16)
    updated = (
        temporal.astype(jnp.float32)
        + jnp.einsum(
            "fbqw,bc->fcqw", back_proj, band_input_weight, preferred_element_type=jnp.float32
        )
    ).astype(jnp.bfloat16)
    cot_hidden = time_mix(cot_space, flipped).astype(jnp.bfloat16)
    gate_grad = (slope * cot_hidden.astype(jnp.float32)).astype(jnp.bfloat16)
    kernel_flip = jnp.transpose(conv_weight[::-1, ::-1], (0, 1, 3, 2))
    features_grad = (cot_hidden.astype(jnp.float32) + spatial_conv(gate_grad, kernel_flip)).astype(
        jnp.bfloat16
    )
    return (updated, features_grad)


def solution(mesh):
    return jax.shard_map(
        on_device,
        mesh=mesh,
        in_specs=(
            P(None, None, "row", ("ta", "col")),
            P(),
            P(),
            P(),
            P(),
            P(("ta", "col"), "row", None),
            P(("ta", "col"), "row", None),
            P(),
            P(("ta", "col"), None, "row", None),
        ),
        out_specs=(P(("ta", "col"), None, "row", None), P(None, None, "row", ("ta", "col"))),
        check_vma=False,
    )
```

```python
import jax
import jax.numpy as jnp
from jax import lax
from jax.sharding import PartitionSpec as P


def with_halo(array, sides, width):
    for axis, dim in sides:
        devices, length = (lax.axis_size(axis), array.shape[dim])
        up = [(i, (i + 1) % devices) for i in range(devices - 1)]
        down = [(j, i) for i, j in up]
        last = lax.slice_in_dim(array, length - width, length, axis=dim)
        initial = lax.slice_in_dim(array, 0, width, axis=dim)
        before = lax.ppermute(last, axis, up)
        after = lax.ppermute(initial, axis, down)
        array = jnp.concatenate([before, array, after], axis=dim)
    return array


def row_halo(field_in):
    return with_halo(field_in, (("row", 2),), 1)


def halo_conv(rows, kernel):
    padded = with_halo(rows, ((("ta", "col"), 3),), 1)
    return lax.conv_general_dilated(
        padded,
        kernel,
        window_strides=(1, 1),
        padding="VALID",
        dimension_numbers=("NCHW", "HWIO", "NCHW"),
        preferred_element_type=jnp.float32,
    )


def spatial_conv(field_in, kernel):
    return halo_conv(row_halo(field_in), kernel)


def lane_rows(block):
    lanes = 128
    return block.reshape(block.shape[0], -1, lanes)


def to_time(field_in):
    blocks = lax.axis_size(("ta", "col"))
    frames = field_in.shape[0] // blocks
    sent = lane_rows(field_in.reshape((blocks, frames * field_in.shape[1]) + field_in.shape[2:]))
    got = lax.all_to_all(sent, ("ta", "col"), split_axis=0, concat_axis=0, tiled=True)
    got = got.reshape((blocks, frames) + field_in.shape[1:])
    return jnp.moveaxis(got, 0, 3).reshape(
        (frames,) + field_in.shape[1:3] + (blocks * field_in.shape[3],)
    )


def space_blocks(field_in):
    blocks = lax.axis_size(("ta", "col"))
    split = field_in.reshape(field_in.shape[:3] + (blocks, field_in.shape[3] // blocks))
    return lane_rows(jnp.moveaxis(split, 3, 0))


def to_space(sent, like):
    blocks = lax.axis_size(("ta", "col"))
    got = lax.all_to_all(sent, ("ta", "col"), split_axis=0, concat_axis=0, tiled=True)
    return got.reshape((blocks * like.shape[0],) + like.shape[1:3] + (like.shape[3] // blocks,))


def time_mix(frames_in, time_taps):
    frame_count = frames_in.shape[0]
    padded = jnp.pad(frames_in, ((2, 2), (0, 0), (0, 0), (0, 0)))
    summed = jnp.zeros(frames_in.shape, jnp.float32)
    for tap_index in range(5):
        summed = summed + time_taps[None, :, tap_index, None, None] * padded[
            tap_index : tap_index + frame_count
        ].astype(jnp.float32)
    return summed


def gelu_exact(values_in):
    return jax.nn.gelu(values_in, approximate=False)


def shift_bits(dispersion, largest):
    bits = largest.bit_length()
    return [((dispersion >> k) & 1).astype(bool)[None, :, None, None] for k in range(bits)]


def disperse(masked, bits, width_wide):
    moved = jnp.pad(masked, ((0, 0),) * 3 + ((0, width_wide - masked.shape[-1]),))
    for k, bit in enumerate(bits):
        step = 1 << k
        later = jnp.pad(moved[..., :-step], ((0, 0),) * 3 + ((step, 0),))
        moved = jnp.where(bit, later, moved)
    return jnp.sum(moved, axis=1)


def undisperse(field_in, bits, width_keep):
    moved = jnp.broadcast_to(
        field_in[:, None], (field_in.shape[0], bits[0].shape[1]) + field_in.shape[1:]
    )
    for k, bit in enumerate(bits):
        step = 1 << k
        earlier = jnp.pad(moved[..., step:], ((0, 0),) * 3 + ((0, step),))
        moved = jnp.where(bit, earlier, moved)
    return moved[..., :width_keep]


def on_device(
    features,
    conv_weight,
    time_weight,
    band_out,
    band_input_weight,
    measured,
    aperture,
    dispersion,
    update_cot,
):
    width_keep = aperture.shape[-1]
    width_wide = measured.shape[-1]
    bits = shift_bits(dispersion, width_wide - width_keep)
    mask_float = aperture.astype(jnp.float32)[:, None]
    band_cot = jnp.einsum(
        "fcqw,bc->fbqw", update_cot, band_input_weight, preferred_element_type=jnp.float32
    )
    resid_grad = disperse(band_cot * mask_float, bits, width_wide)
    band_grad = (-(undisperse(resid_grad, bits, width_keep) * mask_float)).astype(jnp.bfloat16)
    cot_temporal = (
        update_cot.astype(jnp.float32)
        + jnp.einsum("fbqw,cb->fcqw", band_grad, band_out, preferred_element_type=jnp.float32)
    ).astype(jnp.bfloat16)
    feature_rows = row_halo(features)
    feature_rows, cot_sent = lax.optimization_barrier((feature_rows, space_blocks(cot_temporal)))
    pre_act = halo_conv(feature_rows, conv_weight)
    gelu_value, pullback = jax.vjp(gelu_exact, pre_act)
    slope = pullback(jnp.ones_like(pre_act))[0]
    hidden_state = (features.astype(jnp.float32) + gelu_value).astype(jnp.bfloat16)
    temporal_space = time_mix(hidden_state, time_weight).astype(jnp.bfloat16)
    flipped = time_weight[:, ::-1]
    cot_space, slope, temporal_space = lax.optimization_barrier(
        (to_space(cot_sent, cot_temporal), slope, temporal_space)
    )
    temporal = to_time(temporal_space)
    band_vals = jnp.einsum("fcqw,cb->fbqw", temporal, band_out, preferred_element_type=jnp.float32)
    masked_band_sum = disperse(band_vals * mask_float, bits, width_wide)
    residual_error = measured - masked_band_sum
    back_proj = (undisperse(residual_error, bits, width_keep) * mask_float).astype(jnp.bfloat16)
    updated = (
        temporal.astype(jnp.float32)
        + jnp.einsum(
            "fbqw,bc->fcqw", back_proj, band_input_weight, preferred_element_type=jnp.float32
        )
    ).astype(jnp.bfloat16)
    cot_hidden = time_mix(cot_space, flipped).astype(jnp.bfloat16)
    gate_grad = (slope * cot_hidden.astype(jnp.float32)).astype(jnp.bfloat16)
    kernel_flip = jnp.transpose(conv_weight[::-1, ::-1], (0, 1, 3, 2))
    features_grad = (cot_hidden.astype(jnp.float32) + spatial_conv(gate_grad, kernel_flip)).astype(
        jnp.bfloat16
    )
    return (updated, features_grad)


def solution(mesh):
    return jax.shard_map(
        on_device,
        mesh=mesh,
        in_specs=(
            P(None, None, "row", ("ta", "col")),
            P(),
            P(),
            P(),
            P(),
            P(("ta", "col"), "row", None),
            P(("ta", "col"), "row", None),
            P(),
            P(("ta", "col"), None, "row", None),
        ),
        out_specs=(P(("ta", "col"), None, "row", None), P(None, None, "row", ("ta", "col"))),
        check_vma=False,
    )
```
